32 devices in a mesh: groups: 2 (over x), wide: 4 (over y, core), expert: 4 (over z).
Axes of the slice: x: 2, y: 2, z: 4, core: 2. Of those that a mesh axis runs over, the one named last changes fastest.
Arguments:
- prompts: bfloat16 [8, 128, 6144], P(('groups', 'wide'), None, 'expert'), parts along dimension 0, may hold values from -6 to 6
- span_slot_owner: int32 [8], P('groups'), parts along dimension 0, may hold values from 0 to 3, as said below
- row_expert_index: int32 [768, 2], P('groups'), parts along dimension 0, may hold values from 0 to 7, all different within a row
- tile_tenant_index: int32 [6], P('groups'), parts along dimension 0, may hold values from 0 to 7
- tenant_adapter_slot: int32 [16], P('groups'), parts along dimension 0, may hold values from 0 to 7, each once
- router: bfloat16 [6144, 8], replicated, may hold values from -0.078125 to 0.078125
- gate_weight: bfloat16 [2, 6144, 16384], P(None, None, ('wide', 'expert')), may hold values from -0.078125 to 0.078125
- up_weight: bfloat16 [2, 6144, 16384], P(None, None, ('wide', 'expert')), may hold values from -0.078125 to 0.078125
- down_weight: bfloat16 [2, 16384, 6144], P(None, 'wide', 'expert'), may hold values from -0.046875 to 0.046875
- adapter_down_weight: bfloat16 [16, 2, 6144, 64], P(('groups', 'wide'), None, 'expert'), parts along dimension 0, may hold values from -0.078125 to 0.078125
- adapter_up_weight: bfloat16 [16, 2, 64, 16384], P('groups', None, None, ('wide', 'expert')), parts along dimension 0, may hold values from -0.75 to 0.75
Outputs:
- mixed: bfloat16 [768, 6144], P(('groups', 'wide'), 'expert'), parts along dimension 0
The draws below stay inside these ranges and needn't reach their ends.
There are 2 independent parts, one for each index of `groups`. The reference program is written for one: setup_inputs(seed, part) draws one part's arguments, and reference() takes and returns one part's arrays. A program takes and returns all parts, laid end to end along the dimension named above; an argument that names none is the same for every part. Nothing has to cross between parts.
Inputs may be any that keep to these rules, and one draw needn't show every extreme that they name: `span_slot_owner`: a permutation of the slots; span c, for c < 3, is in slot span_slot_owner[c]. `row_expert_index`: each row names two different experts. `tenant_adapter_slot`: a permutation of the slots. `tile_tenant_index`: tenant of rows 128 * i to 128 * i + 127.
All inputs are finite; a program needn't handle non-finite values.
Results may differ from the reference program's by a relative error of at most 0.0051.
Values may be sent and summed in bfloat16 or wider, within the bound.
No kernel may reach another device: no remote copies, remote signals or barrier semaphores. Data moves between devices by JAX's collectives and lax.ppermute only.
A program may use at most 128 MiB of HBM per device.

```python
import math
import jax
import jax.numpy as jnp
import numpy as np
from jax import lax

MODEL_WIDTH = 6144
EXPERT_HIDDEN = 16384
NEXP = 8
TOPK = 2
ADAPTER_RANK = 64
HELD_EXPERTS = 2
SPAN = 128
NCHUNK = 3
TILE = 128
SLOTS = 4
TOKENS = 384
TILES = 3
TENANT_COUNT = 8


def draw_span_slot_owner(key, part):
    order_key = jax.random.fold_in(key, 7)
    pick_key = jax.random.fold_in(key, 11)
    shuffled = jax.random.permutation(order_key, SLOTS).astype(jnp.int32)
    base = jax.random.randint(pick_key, (), 0, SLOTS // 2).astype(jnp.int32)
    target = (2 * base + jnp.asarray(part).astype(jnp.int32)) % SLOTS
    position = jnp.argmax((shuffled == target).astype(jnp.int32)).astype(jnp.int32)
    first_value = shuffled[0]
    swapped = shuffled.at[position].set(first_value)
    swapped = swapped.at[0].set(target)
    return swapped.astype(jnp.int32)


def levels(rng, extent, cuts, low, high):
    loudness = 1.0
    for axis_at, blocks in cuts:
        heights = jax.random.uniform(jax.random.fold_in(jax.random.fold_in(rng, 6), axis_at), (blocks,), jnp.float32, low / len(cuts), high / len(cuts))
        loudness = loudness * jnp.repeat(jnp.exp(heights), extent[axis_at] // blocks).reshape((-1,) + (1,) * (len(extent) - 1 - axis_at))
    return loudness


def cumulative_ranks(number_of, lean):
    weights = [(1 << 20) // math.isqrt(grade ** lean) + 1 for grade in range(1, number_of + 1)]
    spread = 1 + sum(weights) // (1 << 30)
    return np.cumsum(np.array([max(1, weight // spread) for weight in weights]))


def ranked_ids(key, extent, number_of, lean):
    grid = cumulative_ranks(number_of, lean)
    pick = jax.random.randint(jax.random.fold_in(key, 1), extent, 0, int(grid[number_of - 1]))
    grade = jnp.searchsorted(jnp.asarray(grid, jnp.int32), pick, side="right")
    return jax.random.permutation(jax.random.fold_in(key, 2), number_of)[grade].astype(jnp.int32)


def choose_distinct(key, rows, number_of, top, lift):
    ranking = jax.random.permutation(jax.random.fold_in(key, 1), number_of)
    boost = ranking
    for power in range(3):
        boost = boost * boost // number_of
    boost = boost * lift // number_of
    chance = jax.random.randint(jax.random.fold_in(key, 2), (rows, number_of), 0, 4096) + boost
    fixed_rows = jax.random.permutation(jax.random.fold_in(key, 3), rows)[jnp.arange(number_of) % rows]
    chance = jnp.where(jnp.arange(rows)[:, None] == fixed_rows[None, :], 1 << 14, chance)
    priority = chance * number_of + jnp.arange(number_of)
    return lax.top_k(priority.astype(jnp.int32), top)[1].astype(jnp.int32)


def bell_draw(key, dims, spread, reach, shards=(), kind=jnp.bfloat16):
    array = spread * jax.random.normal(key, dims, jnp.float32)
    if shards:
        array = array * levels(key, dims, shards, -0.22, 0.18)
    return jnp.clip(array, -reach, reach).astype(kind)


def setup_inputs(seed: int = 0, part: int = 0) -> dict:
    arg_keys = jax.random.split(jax.random.key(seed), 12)
    part_splits = jax.random.split(jax.random.fold_in(arg_keys[11], part), 12)
    prompts = bell_draw(part_splits[0], (SLOTS, SPAN, MODEL_WIDTH), 1.0, 6.0, ((0, 4), (2, 4)))
    span_slot_owner = draw_span_slot_owner(jax.random.fold_in(jax.random.fold_in(arg_keys[11], part), 71), part)
    row_expert_index = choose_distinct(part_splits[2], TOKENS, NEXP, TOPK, 4096)
    tile_tenant_index = ranked_ids(part_splits[3], (TILES,), TENANT_COUNT, 2)
    tenant_adapter_slot = jax.random.permutation(part_splits[4], TENANT_COUNT).astype(jnp.int32)
    router = bell_draw(arg_keys[5], (MODEL_WIDTH, NEXP), MODEL_WIDTH ** -0.5, 0.078125)
    gate_weight = bell_draw(arg_keys[6], (HELD_EXPERTS, MODEL_WIDTH, EXPERT_HIDDEN), MODEL_WIDTH ** -0.5, 0.078125, ((2, 16),))
    up_weight = bell_draw(arg_keys[7], (HELD_EXPERTS, MODEL_WIDTH, EXPERT_HIDDEN), MODEL_WIDTH ** -0.5, 0.078125, ((2, 16),))
    down_weight = bell_draw(arg_keys[8], (HELD_EXPERTS, EXPERT_HIDDEN, MODEL_WIDTH), EXPERT_HIDDEN ** -0.5, 0.046875, ((1, 4), (2, 4)))
    adapter_down_weight = bell_draw(part_splits[9], (TENANT_COUNT, HELD_EXPERTS, MODEL_WIDTH, ADAPTER_RANK), MODEL_WIDTH ** -0.5, 0.078125, ((0, 4), (2, 4)))
    adapter_up_weight = bell_draw(part_splits[10], (TENANT_COUNT, HELD_EXPERTS, ADAPTER_RANK, EXPERT_HIDDEN), ADAPTER_RANK ** -0.5, 0.75, ((3, 16),))
    return {"prompts": prompts, "span_slot_owner": span_slot_owner, "row_expert_index": row_expert_index, "tile_tenant_index": tile_tenant_index, "tenant_adapter_slot": tenant_adapter_slot, "router": router, "gate_weight": gate_weight, "up_weight": up_weight, "down_weight": down_weight, "adapter_down_weight": adapter_down_weight, "adapter_up_weight": adapter_up_weight}


ADAPTER_SCALE = 0.5


def reference(prompts, span_slot_owner, row_expert_index, tile_tenant_index, tenant_adapter_slot, router, gate_weight, up_weight, down_weight, adapter_down_weight, adapter_up_weight):
    owners = span_slot_owner[:NCHUNK]
    input_rows = jnp.take(prompts, owners, axis=0).reshape(NCHUNK * SPAN, MODEL_WIDTH)
    logits = jnp.dot(input_rows, router, preferred_element_type=jnp.float32)
    chosen = jnp.take_along_axis(logits, row_expert_index, axis=1)
    first_prob = jax.nn.sigmoid(chosen[:, 0] - chosen[:, 1])
    second_prob = jax.nn.sigmoid(chosen[:, 1] - chosen[:, 0])
    tile_slot_index = jnp.take(tenant_adapter_slot, tile_tenant_index)
    down_tile_blocks = jnp.take(adapter_down_weight, tile_slot_index, axis=0).astype(jnp.float32)
    tile_inputs = input_rows.astype(jnp.float32).reshape(TILES, TILE, MODEL_WIDTH)
    lowrank = jnp.einsum("ntd,nedr->nter", tile_inputs, down_tile_blocks).astype(jnp.bfloat16)
    up_tile_blocks = jnp.take(adapter_up_weight, tile_tenant_index, axis=0).astype(jnp.float32)
    adapted_hidden = jnp.einsum("nter,nerf->ntef", lowrank.astype(jnp.float32), up_tile_blocks)
    adapted_hidden = adapted_hidden.reshape(NCHUNK * SPAN, HELD_EXPERTS, EXPERT_HIDDEN)
    running = jnp.zeros((NCHUNK * SPAN, MODEL_WIDTH), jnp.float32)
    for expert_number in range(HELD_EXPERTS):
        weight = first_prob * (row_expert_index[:, 0] == expert_number).astype(jnp.float32)
        weight = weight + second_prob * (row_expert_index[:, 1] == expert_number).astype(jnp.float32)
        gate_pre = jnp.dot(input_rows, gate_weight[expert_number], preferred_element_type=jnp.float32)
        up_projection_value = jnp.dot(input_rows, up_weight[expert_number], preferred_element_type=jnp.float32) + ADAPTER_SCALE * adapted_hidden[:, expert_number]
        hidden = (weight[:, None] * jax.nn.silu(gate_pre) * up_projection_value).astype(jnp.bfloat16)
        running = running + jnp.dot(hidden, down_weight[expert_number], preferred_element_type=jnp.float32)
    return running.astype(jnp.bfloat16)
```

```python
import jax
import jax.numpy as jnp
import numpy as np
from jax import lax
from jax.sharding import Mesh
from jax.sharding import PartitionSpec as P

ADAPTER_SCALE = 0.5

WIDE = ("wy", "wc")
GROUP = ("wy", "wc", "expert")


def per_device(
    prompts,
    span_slot_owner,
    row_expert_index,
    tile_tenant_index,
    tenant_adapter_slot,
    router,
    gate_weight,
    up_weight,
    down_weight,
    adapter_down_weight,
    adapter_up_weight,
):
    span = prompts.shape[1]
    quarter = prompts.shape[2]
    tokens = row_expert_index.shape[0]
    nchunk = tokens // span
    window = gate_weight.shape[0]
    core = lax.axis_index("wc")
    cores = lax.axis_size("wc")
    wide_index = lax.axis_index(WIDE)

    slots_q = lax.all_gather(prompts, WIDE, axis=0, tiled=True)
    rows_q = jnp.take(slots_q, span_slot_owner[:nchunk], axis=0).reshape(tokens, quarter)

    half = tokens // cores
    mine_q = lax.dynamic_slice_in_dim(rows_q, core * half, half, 0)
    mine = lax.all_gather(mine_q, "expert", axis=1, tiled=True)
    input_rows = lax.all_gather(mine, "wc", axis=0, tiled=True)

    logits = jnp.dot(input_rows, router, preferred_element_type=jnp.float32)
    experts = jnp.arange(router.shape[1], dtype=jnp.int32)
    picked = (row_expert_index[:, :, None] == experts[None, None, :]).astype(jnp.float32)
    chosen = jnp.sum(picked * logits[:, None, :], axis=2)
    first_prob = jax.nn.sigmoid(chosen[:, 0] - chosen[:, 1])
    second_prob = jax.nn.sigmoid(chosen[:, 1] - chosen[:, 0])
    weight = (
        first_prob[:, None] * picked[:, 0, :window] + second_prob[:, None] * picked[:, 1, :window]
    )

    tile_count = tile_tenant_index.shape[0]
    tile_rows = tokens // tile_count
    resident_slots = adapter_down_weight.shape[0]
    tile_slot_index = jnp.take(tenant_adapter_slot, tile_tenant_index)
    owners = tile_slot_index // resident_slots
    local_index = tile_slot_index % resident_slots
    held = jnp.take(adapter_down_weight, local_index, axis=0)
    partial_rank = jnp.einsum(
        "ntd,nedr->nter",
        rows_q.reshape(tile_count, tile_rows, quarter),
        held,
        preferred_element_type=jnp.float32,
    )
    partial_rank = jnp.where(
        (owners == wide_index)[:, None, None, None], partial_rank, jnp.zeros_like(partial_rank)
    )
    lowrank = lax.psum(partial_rank, GROUP).astype(jnp.bfloat16)
    tile_up = jnp.take(adapter_up_weight, tile_tenant_index, axis=0)
    adapted_hidden = jnp.einsum(
        "nter,nerf->ntef", lowrank, tile_up, preferred_element_type=jnp.float32
    ).reshape(tokens, window, tile_up.shape[3])

    running = None
    for expert_number in range(window):
        gate_pre = jnp.dot(
            input_rows, gate_weight[expert_number], preferred_element_type=jnp.float32
        )
        up_value = (
            jnp.dot(input_rows, up_weight[expert_number], preferred_element_type=jnp.float32)
            + ADAPTER_SCALE * adapted_hidden[:, expert_number]
        )
        hidden = (
            weight[:, expert_number, None] * jax.nn.silu(gate_pre) * up_value
        ).astype(jnp.bfloat16)
        gathered = lax.all_gather(hidden, "expert", axis=1, tiled=True)
        part = jnp.dot(gathered, down_weight[expert_number], preferred_element_type=jnp.float32)
        running = part if running is None else running + part
    mixed_rows = lax.psum_scatter(running, WIDE, scatter_dimension=0, tiled=True)
    return mixed_rows.astype(jnp.bfloat16)


def solution(mesh):
    groups = mesh.shape["groups"]
    wide = mesh.shape["wide"]
    expert = mesh.shape["expert"]
    split = Mesh(
        np.asarray(mesh.devices).reshape(groups, wide // 2, 2, expert),
        ("groups", "wy", "wc", "expert"),
    )
    rows = ("groups", "wy", "wc")
    in_specs = (
        P(rows, None, "expert"),
        P("groups"),
        P("groups", None),
        P("groups"),
        P("groups"),
        P(),
        P(None, None, GROUP),
        P(None, None, GROUP),
        P(None, WIDE, "expert"),
        P(rows, None, "expert", None),
        P("groups", None, None, GROUP),
    )
    out_specs = P(rows, "expert")
    return jax.shard_map(
        per_device, mesh=split, in_specs=in_specs, out_specs=out_specs, check_vma=False
    )
```

```python
import jax
import jax.numpy as jnp
import numpy as np
from jax import lax
from jax.sharding import Mesh
from jax.sharding import PartitionSpec as P

ADAPTER_SCALE = 0.5

WIDE = ("wy", "wc")
GROUP = ("wy", "wc", "expert")


def per_device(
    prompts,
    span_slot_owner,
    row_expert_index,
    tile_tenant_index,
    tenant_adapter_slot,
    router,
    gate_weight,
    up_weight,
    down_weight,
    adapter_down_weight,
    adapter_up_weight,
):
    span = prompts.shape[1]
    quarter = prompts.shape[2]
    tokens = row_expert_index.shape[0]
    nchunk = tokens // span
    window = gate_weight.shape[0]
    core = lax.axis_index("wc")
    cores = lax.axis_size("wc")
    wide_index = lax.axis_index(WIDE)

    slots_q = lax.all_gather(prompts, WIDE, axis=0, tiled=True)
    rows_q = jnp.take(slots_q, span_slot_owner[:nchunk], axis=0).reshape(tokens, quarter)

    half = tokens // cores
    mine_q = lax.dynamic_slice_in_dim(rows_q, core * half, half, 0)
    mine = lax.all_gather(mine_q, "expert", axis=1, tiled=True)
    other = lax.ppermute(mine, "wc", [(i, (i + 1) % cores) for i in range(cores)])
    first = jnp.where(core == 0, mine, other)
    second = jnp.where(core == 0, other, mine)
    input_rows = jnp.concatenate([first, second], axis=0)

    logits = jnp.dot(input_rows, router, preferred_element_type=jnp.float32)
    experts = jnp.arange(router.shape[1], dtype=jnp.int32)
    picked = (row_expert_index[:, :, None] == experts[None, None, :]).astype(jnp.float32)
    chosen = jnp.sum(picked * logits[:, None, :], axis=2)
    first_prob = jax.nn.sigmoid(chosen[:, 0] - chosen[:, 1])
    second_prob = jax.nn.sigmoid(chosen[:, 1] - chosen[:, 0])
    weight = (
        first_prob[:, None] * picked[:, 0, :window] + second_prob[:, None] * picked[:, 1, :window]
    )

    tile_count = tile_tenant_index.shape[0]
    tile_rows = tokens // tile_count
    resident_slots = adapter_down_weight.shape[0]
    tile_slot_index = jnp.take(tenant_adapter_slot, tile_tenant_index)
    owners = tile_slot_index // resident_slots
    local_index = tile_slot_index % resident_slots
    held = jnp.take(adapter_down_weight, local_index, axis=0)
    partial_rank = jnp.einsum(
        "ntd,nedr->nter",
        rows_q.reshape(tile_count, tile_rows, quarter),
        held,
        preferred_element_type=jnp.float32,
    )
    partial_rank = jnp.where(
        (owners == wide_index)[:, None, None, None], partial_rank, jnp.zeros_like(partial_rank)
    )
    lowrank = lax.reduce_precision(lax.psum(partial_rank, GROUP), exponent_bits=8, mantissa_bits=7)
    tile_up = jnp.take(adapter_up_weight, tile_tenant_index, axis=0)
    adapted_hidden = jnp.einsum(
        "nter,nerf->ntef", lowrank, tile_up.astype(jnp.float32), preferred_element_type=jnp.float32
    ).reshape(tokens, window, tile_up.shape[3])

    running = None
    for expert_number in range(window):
        gate_pre = jnp.dot(
            input_rows, gate_weight[expert_number], preferred_element_type=jnp.float32
        )
        up_value = (
            jnp.dot(input_rows, up_weight[expert_number], preferred_element_type=jnp.float32)
            + ADAPTER_SCALE * adapted_hidden[:, expert_number]
        )
        hidden = (
            weight[:, expert_number, None] * jax.nn.silu(gate_pre) * up_value
        ).astype(jnp.bfloat16)
        gathered = lax.all_gather(hidden, "expert", axis=1, tiled=True)
        part = jnp.dot(gathered, down_weight[expert_number], preferred_element_type=jnp.float32)
        running = part if running is None else running + part
    mixed_rows = lax.psum_scatter(running, WIDE, scatter_dimension=0, tiled=True)
    return mixed_rows.astype(jnp.bfloat16)


def solution(mesh):
    groups = mesh.shape["groups"]
    wide = mesh.shape["wide"]
    expert = mesh.shape["expert"]
    split = Mesh(
        np.asarray(mesh.devices).reshape(groups, wide // 2, 2, expert),
        ("groups", "wy", "wc", "expert"),
    )
    rows = ("groups", "wy", "wc")
    in_specs = (
        P(rows, None, "expert"),
        P("groups"),
        P("groups", None),
        P("groups"),
        P("groups"),
        P(),
        P(None, None, GROUP),
        P(None, None, GROUP),
        P(None, WIDE, "expert"),
        P(rows, None, "expert", None),
        P("groups", None, None, GROUP),
    )
    out_specs = P(rows, "expert")
    return jax.shard_map(
        per_device, mesh=split, in_specs=in_specs, out_specs=out_specs, check_vma=False
    )
```

```python
import jax
import jax.numpy as jnp
import numpy as np
from jax import lax
from jax.sharding import Mesh
from jax.sharding import PartitionSpec as P

ADAPTER_SCALE = 0.5

WIDE = ("wy", "wc")
GROUP = ("wy", "wc", "expert")


def per_device(
    prompts,
    span_slot_owner,
    row_expert_index,
    tile_tenant_index,
    tenant_adapter_slot,
    router,
    gate_weight,
    up_weight,
    down_weight,
    adapter_down_weight,
    adapter_up_weight,
):
    span = prompts.shape[1]
    quarter = prompts.shape[2]
    tokens = row_expert_index.shape[0]
    nchunk = tokens // span
    window = gate_weight.shape[0]
    core = lax.axis_index("wc")
    cores = lax.axis_size("wc")
    wide_index = lax.axis_index(WIDE)

    tile_count = tile_tenant_index.shape[0]
    tile_rows = tokens // tile_count
    resident_slots = adapter_down_weight.shape[0]
    rank = adapter_down_weight.shape[3]
    held = jnp.transpose(adapter_down_weight, (0, 1, 3, 2)).reshape(-1, quarter)
    packed = jnp.concatenate([prompts.reshape(-1, quarter), held], axis=0)
    gathered_q = lax.all_gather(packed, WIDE, axis=0, tiled=False)
    wide_size = gathered_q.shape[0]
    slot_rows = prompts.shape[0] * span
    slots_q = gathered_q[:, :slot_rows]
    adapters_q = gathered_q[:, slot_rows:].reshape(wide_size * resident_slots, window, rank, quarter)
    slot_of_span = span_slot_owner[:nchunk]
    rows_q = jnp.take(slots_q.reshape(-1, span, quarter), slot_of_span, axis=0).reshape(tokens, quarter)

    tile_slot_index = jnp.take(tenant_adapter_slot, tile_tenant_index)
    tile_adapters = jnp.take(adapters_q, tile_slot_index, axis=0)
    partial_rank = jnp.einsum(
        "ntd,nerd->nter",
        rows_q.reshape(tile_count, tile_rows, quarter),
        tile_adapters,
        preferred_element_type=jnp.float32,
    ).reshape(tokens, window * rank)
    rank_hi = partial_rank.astype(jnp.bfloat16)
    rank_lo = (partial_rank - rank_hi.astype(jnp.float32)).astype(jnp.bfloat16)

    half = tokens // cores
    mine_q = jnp.concatenate([rows_q, rank_hi, rank_lo], axis=1)
    mine_q = lax.dynamic_slice_in_dim(mine_q, core * half, half, 0)
    expert_size = lax.axis_size("expert")
    arrived = lax.all_gather(mine_q, "expert", axis=1, tiled=False)
    mine = arrived[:, :, :quarter].reshape(half, expert_size * quarter)
    pieces = arrived[:, :, quarter:].astype(jnp.float32)
    summed = jnp.sum(pieces[:, :, : window * rank] + pieces[:, :, window * rank :], axis=1)
    mine_rank = summed.astype(jnp.bfloat16)
    mine = jnp.concatenate([mine, mine_rank], axis=1)
    other = lax.ppermute(mine, "wc", [(i, (i + 1) % cores) for i in range(cores)])
    first = jnp.where(core == 0, mine, other)
    second = jnp.where(core == 0, other, mine)
    both = jnp.concatenate([first, second], axis=0)
    input_rows = both[:, : expert_size * quarter]
    lowrank = both[:, expert_size * quarter :].reshape(tile_count, tile_rows, window, rank)

    logits = jnp.dot(input_rows, router, preferred_element_type=jnp.float32)
    experts = jnp.arange(router.shape[1], dtype=jnp.int32)
    picked = (row_expert_index[:, :, None] == experts[None, None, :]).astype(jnp.float32)
    chosen = jnp.sum(picked * logits[:, None, :], axis=2)
    first_prob = jax.nn.sigmoid(chosen[:, 0] - chosen[:, 1])
    second_prob = jax.nn.sigmoid(chosen[:, 1] - chosen[:, 0])
    weight = (
        first_prob[:, None] * picked[:, 0, :window] + second_prob[:, None] * picked[:, 1, :window]
    )

    tile_up = jnp.take(adapter_up_weight, tile_tenant_index, axis=0)
    adapted_hidden = jnp.einsum(
        "nter,nerf->ntef", lowrank, tile_up, preferred_element_type=jnp.float32
    ).reshape(tokens, window, tile_up.shape[3])

    running = None
    for expert_number in range(window):
        gate_pre = jnp.dot(
            input_rows, gate_weight[expert_number], preferred_element_type=jnp.float32
        )
        up_value = (
            jnp.dot(input_rows, up_weight[expert_number], preferred_element_type=jnp.float32)
            + ADAPTER_SCALE * adapted_hidden[:, expert_number]
        )
        hidden = (
            weight[:, expert_number, None] * jax.nn.silu(gate_pre) * up_value
        ).astype(jnp.bfloat16)
        gathered = lax.all_gather(hidden, "expert", axis=1, tiled=True)
        part = jnp.dot(gathered, down_weight[expert_number], preferred_element_type=jnp.float32)
        running = part if running is None else running + part
    mixed_rows = lax.psum_scatter(running, WIDE, scatter_dimension=0, tiled=True)
    return mixed_rows.astype(jnp.bfloat16)


def solution(mesh):
    groups = mesh.shape["groups"]
    wide = mesh.shape["wide"]
    expert = mesh.shape["expert"]
    split = Mesh(
        np.asarray(mesh.devices).reshape(groups, wide // 2, 2, expert),
        ("groups", "wy", "wc", "expert"),
    )
    rows = ("groups", "wy", "wc")
    in_specs = (
        P(rows, None, "expert"),
        P("groups"),
        P("groups", None),
        P("groups"),
        P("groups"),
        P(),
        P(None, None, GROUP),
        P(None, None, GROUP),
        P(None, WIDE, "expert"),
        P(rows, None, "expert", None),
        P("groups", None, None, GROUP),
    )
    out_specs = P(rows, "expert")
    return jax.shard_map(
        per_device, mesh=split, in_specs=in_specs, out_specs=out_specs, check_vma=False
    )
```

```python
import jax
import jax.numpy as jnp
import numpy as np
from jax import lax
from jax.sharding import Mesh
from jax.sharding import PartitionSpec as P

ADAPTER_SCALE = 0.5

WIDE = ("wy", "wc")
GROUP = ("wy", "wc", "expert")


def per_device(
    prompts,
    span_slot_owner,
    row_expert_index,
    tile_tenant_index,
    tenant_adapter_slot,
    router,
    gate_weight,
    up_weight,
    down_weight,
    adapter_down_weight,
    adapter_up_weight,
):
    span = prompts.shape[1]
    quarter = prompts.shape[2]
    tokens = row_expert_index.shape[0]
    nchunk = tokens // span
    window = gate_weight.shape[0]
    core = lax.axis_index("wc")
    cores = lax.axis_size("wc")
    wide_index = lax.axis_index(WIDE)

    tile_count = tile_tenant_index.shape[0]
    tile_rows = tokens // tile_count
    resident_slots = adapter_down_weight.shape[0]
    rank = adapter_down_weight.shape[3]
    held = jnp.transpose(adapter_down_weight, (0, 1, 3, 2)).reshape(-1, quarter)
    packed = jnp.concatenate([prompts.reshape(-1, quarter), held], axis=0)
    gathered_q = lax.all_gather(packed, WIDE, axis=0, tiled=False)
    wide_size = gathered_q.shape[0]
    slot_rows = prompts.shape[0] * span
    slots_q = gathered_q[:, :slot_rows]
    adapters_q = gathered_q[:, slot_rows:].reshape(wide_size * resident_slots, window, rank, quarter)
    slot_of_span = span_slot_owner[:nchunk]
    rows_q = jnp.take(slots_q.reshape(-1, span, quarter), slot_of_span, axis=0).reshape(tokens, quarter)

    tile_slot_index = jnp.take(tenant_adapter_slot, tile_tenant_index)
    tile_adapters = jnp.take(adapters_q, tile_slot_index, axis=0)
    partial_rank = jnp.einsum(
        "ntd,nerd->nter",
        rows_q.reshape(tile_count, tile_rows, quarter),
        tile_adapters,
        preferred_element_type=jnp.float32,
    ).reshape(tokens, window * rank)
    rank_top = lax.reduce_precision(partial_rank, exponent_bits=8, mantissa_bits=7)
    rank_hi = rank_top.astype(jnp.bfloat16)
    rank_lo = (partial_rank - rank_top).astype(jnp.bfloat16)

    half = tokens // cores
    mine_q = jnp.concatenate([rows_q, rank_hi, rank_lo], axis=1)
    mine_q = lax.dynamic_slice_in_dim(mine_q, core * half, half, 0)
    expert_size = lax.axis_size("expert")
    arrived = lax.all_gather(mine_q, "expert", axis=1, tiled=False)
    mine = arrived[:, :, :quarter].reshape(half, expert_size * quarter)
    pieces = arrived[:, :, quarter:].astype(jnp.float32)
    summed = jnp.sum(pieces[:, :, : window * rank] + pieces[:, :, window * rank :], axis=1)
    mine_rank = summed.astype(jnp.bfloat16)
    mine = jnp.concatenate([mine, mine_rank], axis=1)
    other = lax.ppermute(mine, "wc", [(i, (i + 1) % cores) for i in range(cores)])
    first = jnp.where(core == 0, mine, other)
    second = jnp.where(core == 0, other, mine)
    both = jnp.concatenate([first, second], axis=0)
    input_rows = both[:, : expert_size * quarter]
    lowrank = both[:, expert_size * quarter :].reshape(tile_count, tile_rows, window, rank)

    logits = jnp.dot(input_rows, router, preferred_element_type=jnp.float32)
    experts = jnp.arange(router.shape[1], dtype=jnp.int32)
    picked = (row_expert_index[:, :, None] == experts[None, None, :]).astype(jnp.float32)
    chosen = jnp.sum(picked * logits[:, None, :], axis=2)
    first_prob = jax.nn.sigmoid(chosen[:, 0] - chosen[:, 1])
    second_prob = jax.nn.sigmoid(chosen[:, 1] - chosen[:, 0])
    weight = (
        first_prob[:, None] * picked[:, 0, :window] + second_prob[:, None] * picked[:, 1, :window]
    )

    tile_up = jnp.take(adapter_up_weight, tile_tenant_index, axis=0)
    adapted_hidden = jnp.einsum(
        "nter,nerf->ntef", lowrank, tile_up, preferred_element_type=jnp.float32
    ).reshape(tokens, window, tile_up.shape[3])

    pieces_per_expert = 2
    units = gate_weight.shape[2]
    piece = units // pieces_per_expert
    expert_size = lax.axis_size("expert")
    reduced = None
    for expert_number in range(window):
        running = None
        for piece_number in range(pieces_per_expert):
            cols = slice(piece_number * piece, (piece_number + 1) * piece)
            gate_pre = jnp.dot(
                input_rows, gate_weight[expert_number, :, cols], preferred_element_type=jnp.float32
            )
            up_value = (
                jnp.dot(
                    input_rows, up_weight[expert_number, :, cols], preferred_element_type=jnp.float32
                )
                + ADAPTER_SCALE * adapted_hidden[:, expert_number, cols]
            )
            hidden = (
                weight[:, expert_number, None] * jax.nn.silu(gate_pre) * up_value
            ).astype(jnp.bfloat16)
            gathered = lax.all_gather(hidden, "expert", axis=1, tiled=False)
            down_rows = down_weight[expert_number].reshape(expert_size, units, -1)[:, cols]
            part = jnp.einsum(
                "tef,efd->td", gathered, down_rows, preferred_element_type=jnp.float32
            )
            running = part if running is None else running + part
        rows_sum = reduce_rows(running, core, cores)
        reduced = rows_sum if reduced is None else reduced + rows_sum
    return reduced.astype(jnp.bfloat16)


def reduce_rows(running, core, cores):
    chips = lax.axis_size("wy")
    block = running.shape[0] // (chips * cores)
    by_chip = running.reshape(chips, cores, block, running.shape[1])
    keep = jnp.where(core == 0, by_chip[:, 0], by_chip[:, 1])
    send = jnp.where(core == 0, by_chip[:, 1], by_chip[:, 0])
    chip_sum = keep + lax.ppermute(send, "wc", [(i, (i + 1) % cores) for i in range(cores)])
    if chips == 2:
        chip = lax.axis_index("wy")
        mine = jnp.where(chip == 0, chip_sum[0], chip_sum[1])
        away = jnp.where(chip == 0, chip_sum[1], chip_sum[0])
        return mine + lax.ppermute(away, "wy", [(0, 1), (1, 0)])
    return lax.psum_scatter(chip_sum, "wy", scatter_dimension=0, tiled=True).reshape(block, -1)


def solution(mesh):
    groups = mesh.shape["groups"]
    wide = mesh.shape["wide"]
    expert = mesh.shape["expert"]
    split = Mesh(
        np.asarray(mesh.devices).reshape(groups, wide // 2, 2, expert),
        ("groups", "wy", "wc", "expert"),
    )
    rows = ("groups", "wy", "wc")
    in_specs = (
        P(rows, None, "expert"),
        P("groups"),
        P("groups", None),
        P("groups"),
        P("groups"),
        P(),
        P(None, None, GROUP),
        P(None, None, GROUP),
        P(None, WIDE, "expert"),
        P(rows, None, "expert", None),
        P("groups", None, None, GROUP),
    )
    out_specs = P(rows, "expert")
    return jax.shard_map(
        per_device, mesh=split, in_specs=in_specs, out_specs=out_specs, check_vma=False
    )
```

```python
import jax
import jax.numpy as jnp
import numpy as np
from jax import lax
from jax.sharding import Mesh
from jax.sharding import PartitionSpec as P

ADAPTER_SCALE = 0.5

WIDE = ("wy", "wc")
GROUP = ("wy", "wc", "expert")


def per_device(
    prompts,
    span_slot_owner,
    row_expert_index,
    tile_tenant_index,
    tenant_adapter_slot,
    router,
    gate_weight,
    up_weight,
    down_weight,
    adapter_down_weight,
    adapter_up_weight,
):
    span = prompts.shape[1]
    quarter = prompts.shape[2]
    tokens = row_expert_index.shape[0]
    nchunk = tokens // span
    window = gate_weight.shape[0]
    core = lax.axis_index("wc")
    cores = lax.axis_size("wc")
    wide_index = lax.axis_index(WIDE)

    tile_count = tile_tenant_index.shape[0]
    tile_rows = tokens // tile_count
    resident_slots = adapter_down_weight.shape[0]
    rank = adapter_down_weight.shape[3]
    held = jnp.transpose(adapter_down_weight, (0, 1, 3, 2)).reshape(-1, quarter)
    packed = jnp.concatenate([prompts.reshape(-1, quarter), held], axis=0)
    gathered_q = lax.all_gather(packed, WIDE, axis=0, tiled=False)
    wide_size = gathered_q.shape[0]
    slot_rows = prompts.shape[0] * span
    slots_q = gathered_q[:, :slot_rows]
    adapters_q = gathered_q[:, slot_rows:].reshape(wide_size * resident_slots, window, rank, quarter)
    slot_of_span = span_slot_owner[:nchunk]
    rows_q = jnp.take(slots_q.reshape(-1, span, quarter), slot_of_span, axis=0).reshape(tokens, quarter)

    tile_slot_index = jnp.take(tenant_adapter_slot, tile_tenant_index)
    tile_adapters = jnp.take(adapters_q, tile_slot_index, axis=0)
    partial_rank = jnp.einsum(
        "ntd,nerd->nter",
        rows_q.reshape(tile_count, tile_rows, quarter),
        tile_adapters,
        preferred_element_type=jnp.float32,
    ).reshape(tokens, window * rank)
    rank_top = lax.reduce_precision(partial_rank, exponent_bits=8, mantissa_bits=7)
    rank_hi = rank_top.astype(jnp.bfloat16)
    rank_lo = (partial_rank - rank_top).astype(jnp.bfloat16)

    half = tokens // cores
    mine_q = jnp.concatenate([rows_q, rank_hi, rank_lo], axis=1)
    mine_q = lax.dynamic_slice_in_dim(mine_q, core * half, half, 0)
    expert_size = lax.axis_size("expert")
    arrived = lax.all_gather(mine_q, "expert", axis=1, tiled=False)
    mine = arrived[:, :, :quarter].reshape(half, expert_size * quarter)
    pieces = arrived[:, :, quarter:].astype(jnp.float32)
    summed = jnp.sum(pieces[:, :, : window * rank] + pieces[:, :, window * rank :], axis=1)
    mine_rank = summed.astype(jnp.bfloat16)
    mine = jnp.concatenate([mine, mine_rank], axis=1)
    other = lax.ppermute(mine, "wc", [(i, (i + 1) % cores) for i in range(cores)])
    first = jnp.where(core == 0, mine, other)
    second = jnp.where(core == 0, other, mine)
    both = jnp.concatenate([first, second], axis=0)
    input_rows = both[:, : expert_size * quarter]
    lowrank = both[:, expert_size * quarter :].reshape(tile_count, tile_rows, window, rank)

    logits = jnp.dot(input_rows, router, preferred_element_type=jnp.float32)
    experts = jnp.arange(router.shape[1], dtype=jnp.int32)
    picked = (row_expert_index[:, :, None] == experts[None, None, :]).astype(jnp.float32)
    chosen = jnp.sum(picked * logits[:, None, :], axis=2)
    first_prob = jax.nn.sigmoid(chosen[:, 0] - chosen[:, 1])
    second_prob = jax.nn.sigmoid(chosen[:, 1] - chosen[:, 0])
    weight = (
        first_prob[:, None] * picked[:, 0, :window] + second_prob[:, None] * picked[:, 1, :window]
    )

    tile_up = jnp.take(adapter_up_weight, tile_tenant_index, axis=0)
    adapted_hidden = jnp.einsum(
        "nter,nerf->ntef", lowrank, tile_up, preferred_element_type=jnp.float32
    ).reshape(tokens, window, tile_up.shape[3])

    running = None
    for expert_number in range(window):
        gate_pre = jnp.dot(
            input_rows, gate_weight[expert_number], preferred_element_type=jnp.float32
        )
        up_value = (
            jnp.dot(input_rows, up_weight[expert_number], preferred_element_type=jnp.float32)
            + ADAPTER_SCALE * adapted_hidden[:, expert_number]
        )
        hidden = (
            weight[:, expert_number, None] * jax.nn.silu(gate_pre) * up_value
        ).astype(jnp.bfloat16)
        gathered = lax.all_gather(hidden, "expert", axis=1, tiled=True)
        part = jnp.dot(gathered, down_weight[expert_number], preferred_element_type=jnp.float32)
        running = part if running is None else running + part
    return reduce_rows(running, core, cores).astype(jnp.bfloat16)


def reduce_rows(running, core, cores):
    chips = lax.axis_size("wy")
    block = running.shape[0] // (chips * cores)
    by_chip = running.reshape(chips, cores, block, running.shape[1])
    keep = jnp.where(core == 0, by_chip[:, 0], by_chip[:, 1])
    send = jnp.where(core == 0, by_chip[:, 1], by_chip[:, 0])
    chip_sum = keep + lax.ppermute(send, "wc", [(i, (i + 1) % cores) for i in range(cores)])
    if chips == 2:
        chip = lax.axis_index("wy")
        mine = jnp.where(chip == 0, chip_sum[0], chip_sum[1])
        away = jnp.where(chip == 0, chip_sum[1], chip_sum[0])
        return mine + lax.ppermute(away, "wy", [(0, 1), (1, 0)])
    return lax.psum_scatter(chip_sum, "wy", scatter_dimension=0, tiled=True).reshape(block, -1)


def solution(mesh):
    groups = mesh.shape["groups"]
    wide = mesh.shape["wide"]
    expert = mesh.shape["expert"]
    split = Mesh(
        np.asarray(mesh.devices).reshape(groups, wide // 2, 2, expert),
        ("groups", "wy", "wc", "expert"),
    )
    rows = ("groups", "wy", "wc")
    in_specs = (
        P(rows, None, "expert"),
        P("groups"),
        P("groups", None),
        P("groups"),
        P("groups"),
        P(),
        P(None, None, GROUP),
        P(None, None, GROUP),
        P(None, WIDE, "expert"),
        P(rows, None, "expert", None),
        P("groups", None, None, GROUP),
    )
    out_specs = P(rows, "expert")
    return jax.shard_map(
        per_device, mesh=split, in_specs=in_specs, out_specs=out_specs, check_vma=False
    )
```

```python
import jax
import jax.numpy as jnp
import numpy as np
from jax import lax
from jax.sharding import Mesh
from jax.sharding import PartitionSpec as P

ADAPTER_SCALE = 0.5

WIDE = ("wy", "wc")
GROUP = ("wy", "wc", "expert")


def per_device(
    prompts,
    span_slot_owner,
    row_expert_index,
    tile_tenant_index,
    tenant_adapter_slot,
    router,
    gate_weight,
    up_weight,
    down_weight,
    adapter_down_weight,
    adapter_up_weight,
):
    span = prompts.shape[1]
    quarter = prompts.shape[2]
    tokens = row_expert_index.shape[0]
    nchunk = tokens // span
    window = gate_weight.shape[0]
    core = lax.axis_index("wc")
    cores = lax.axis_size("wc")
    wide_index = lax.axis_index(WIDE)

    tile_count = tile_tenant_index.shape[0]
    tile_rows = tokens // tile_count
    resident_slots = adapter_down_weight.shape[0]
    rank = adapter_down_weight.shape[3]
    slots_q = lax.all_gather(prompts, WIDE, axis=0, tiled=True)
    slot_of_span = span_slot_owner[:nchunk]
    rows_q = jnp.take(slots_q, slot_of_span, axis=0).reshape(tokens, quarter)

    chips = lax.axis_size("wy")
    tile_slot_index = jnp.take(tenant_adapter_slot, tile_tenant_index)
    holder = tile_slot_index // resident_slots
    local_slot = tile_slot_index % resident_slots
    if chips == 2 and cores == 2:
        swap = [(0, 1), (1, 0)]
        from_chip = lax.ppermute(adapter_down_weight, "wy", swap)
        from_core = lax.ppermute(adapter_down_weight, "wc", swap)
        from_both = lax.ppermute(from_chip, "wc", swap)
        stacked = jnp.stack([adapter_down_weight, from_core, from_chip, from_both])
        source = jnp.bitwise_xor(holder, wide_index)
    else:
        stacked = lax.all_gather(adapter_down_weight, WIDE, axis=0, tiled=False)
        source = holder
    flat_held = stacked.reshape((-1,) + adapter_down_weight.shape[1:])
    tile_adapters = jnp.take(flat_held, source * resident_slots + local_slot, axis=0)

    partial_rank = jnp.einsum(
        "ntd,nedr->nter",
        rows_q.reshape(tile_count, tile_rows, quarter),
        tile_adapters,
        preferred_element_type=jnp.float32,
    ).reshape(tokens, window * rank)
    rank_top = lax.reduce_precision(partial_rank, exponent_bits=8, mantissa_bits=7)
    rank_hi = rank_top.astype(jnp.bfloat16)
    rank_lo = (partial_rank - rank_top).astype(jnp.bfloat16)

    half = tokens // cores
    mine_q = jnp.concatenate([rows_q, rank_hi, rank_lo], axis=1)
    mine_q = lax.dynamic_slice_in_dim(mine_q, core * half, half, 0)
    expert_size = lax.axis_size("expert")
    arrived = lax.all_gather(mine_q, "expert", axis=1, tiled=False)
    mine = arrived[:, :, :quarter].reshape(half, expert_size * quarter)
    pieces = arrived[:, :, quarter:].astype(jnp.float32)
    summed = jnp.sum(pieces[:, :, : window * rank] + pieces[:, :, window * rank :], axis=1)
    mine_rank = summed.astype(jnp.bfloat16)
    mine = jnp.concatenate([mine, mine_rank], axis=1)
    other = lax.ppermute(mine, "wc", [(i, (i + 1) % cores) for i in range(cores)])
    first = jnp.where(core == 0, mine, other)
    second = jnp.where(core == 0, other, mine)
    both = jnp.concatenate([first, second], axis=0)
    input_rows = both[:, : expert_size * quarter]
    lowrank = both[:, expert_size * quarter :].reshape(tile_count, tile_rows, window, rank)

    logits = jnp.dot(input_rows, router, preferred_element_type=jnp.float32)
    experts = jnp.arange(router.shape[1], dtype=jnp.int32)
    picked = (row_expert_index[:, :, None] == experts[None, None, :]).astype(jnp.float32)
    chosen = jnp.sum(picked * logits[:, None, :], axis=2)
    first_prob = jax.nn.sigmoid(chosen[:, 0] - chosen[:, 1])
    second_prob = jax.nn.sigmoid(chosen[:, 1] - chosen[:, 0])
    weight = (
        first_prob[:, None] * picked[:, 0, :window] + second_prob[:, None] * picked[:, 1, :window]
    )

    tile_up = jnp.take(adapter_up_weight, tile_tenant_index, axis=0)
    adapted_hidden = jnp.einsum(
        "nter,nerf->ntef", lowrank, tile_up, preferred_element_type=jnp.float32
    ).reshape(tokens, window, tile_up.shape[3])

    running = None
    for expert_number in range(window):
        gate_pre = jnp.dot(
            input_rows, gate_weight[expert_number], preferred_element_type=jnp.float32
        )
        up_value = (
            jnp.dot(input_rows, up_weight[expert_number], preferred_element_type=jnp.float32)
            + ADAPTER_SCALE * adapted_hidden[:, expert_number]
        )
        hidden = (
            weight[:, expert_number, None] * jax.nn.silu(gate_pre) * up_value
        ).astype(jnp.bfloat16)
        gathered = lax.all_gather(hidden, "expert", axis=1, tiled=True)
        part = jnp.dot(gathered, down_weight[expert_number], preferred_element_type=jnp.float32)
        running = part if running is None else running + part
    return reduce_rows(running, core, cores).astype(jnp.bfloat16)


def reduce_rows(running, core, cores):
    chips = lax.axis_size("wy")
    block = running.shape[0] // (chips * cores)
    by_chip = running.reshape(chips, cores, block, running.shape[1])
    keep = jnp.where(core == 0, by_chip[:, 0], by_chip[:, 1])
    send = jnp.where(core == 0, by_chip[:, 1], by_chip[:, 0])
    chip_sum = keep + lax.ppermute(send, "wc", [(i, (i + 1) % cores) for i in range(cores)])
    if chips == 2:
        chip = lax.axis_index("wy")
        mine = jnp.where(chip == 0, chip_sum[0], chip_sum[1])
        away = jnp.where(chip == 0, chip_sum[1], chip_sum[0])
        return mine + lax.ppermute(away, "wy", [(0, 1), (1, 0)])
    return lax.psum_scatter(chip_sum, "wy", scatter_dimension=0, tiled=True).reshape(block, -1)


def solution(mesh):
    groups = mesh.shape["groups"]
    wide = mesh.shape["wide"]
    expert = mesh.shape["expert"]
    split = Mesh(
        np.asarray(mesh.devices).reshape(groups, wide // 2, 2, expert),
        ("groups", "wy", "wc", "expert"),
    )
    rows = ("groups", "wy", "wc")
    in_specs = (
        P(rows, None, "expert"),
        P("groups"),
        P("groups", None),
        P("groups"),
        P("groups"),
        P(),
        P(None, None, GROUP),
        P(None, None, GROUP),
        P(None, WIDE, "expert"),
        P(rows, None, "expert", None),
        P("groups", None, None, GROUP),
    )
    out_specs = P(rows, "expert")
    return jax.shard_map(
        per_device, mesh=split, in_specs=in_specs, out_specs=out_specs, check_vma=False
    )
```

```python
import jax
import jax.numpy as jnp
import numpy as np
from jax import lax
from jax.sharding import Mesh
from jax.sharding import PartitionSpec as P

ADAPTER_SCALE = 0.5

WIDE = ("wy", "wc")
GROUP = ("wy", "wc", "expert")


def per_device(
    prompts,
    span_slot_owner,
    row_expert_index,
    tile_tenant_index,
    tenant_adapter_slot,
    router,
    gate_weight,
    up_weight,
    down_weight,
    adapter_down_weight,
    adapter_up_weight,
):
    span = prompts.shape[1]
    quarter = prompts.shape[2]
    tokens = row_expert_index.shape[0]
    nchunk = tokens // span
    window = gate_weight.shape[0]
    core = lax.axis_index("wc")
    cores = lax.axis_size("wc")
    wide_index = lax.axis_index(WIDE)

    tile_count = tile_tenant_index.shape[0]
    tile_rows = tokens // tile_count
    resident_slots = adapter_down_weight.shape[0]
    rank = adapter_down_weight.shape[3]
    slots_q = lax.all_gather(prompts, WIDE, axis=0, tiled=True)
    slot_of_span = span_slot_owner[:nchunk]
    rows_q = jnp.take(slots_q, slot_of_span, axis=0).reshape(tokens, quarter)

    chips = lax.axis_size("wy")
    tile_slot_index = jnp.take(tenant_adapter_slot, tile_tenant_index)
    holder = tile_slot_index // resident_slots
    local_slot = tile_slot_index % resident_slots
    if chips == 2 and cores == 2:
        swap = [(0, 1), (1, 0)]
        from_chip = lax.ppermute(adapter_down_weight, "wy", swap)
        from_core = lax.ppermute(adapter_down_weight, "wc", swap)
        from_both = lax.ppermute(from_chip, "wc", swap)
        stacked = jnp.stack([adapter_down_weight, from_core, from_chip, from_both])
        source = jnp.bitwise_xor(holder, wide_index)
    else:
        stacked = lax.all_gather(adapter_down_weight, WIDE, axis=0, tiled=False)
        source = holder
    flat_held = stacked.reshape((-1,) + adapter_down_weight.shape[1:])
    tile_adapters = jnp.take(flat_held, source * resident_slots + local_slot, axis=0)

    partial_rank = jnp.einsum(
        "ntd,nedr->nter",
        rows_q.reshape(tile_count, tile_rows, quarter),
        tile_adapters,
        preferred_element_type=jnp.float32,
    ).reshape(tokens, window * rank)
    rank_top = lax.reduce_precision(partial_rank, exponent_bits=8, mantissa_bits=7)
    rank_hi = rank_top.astype(jnp.bfloat16)
    rank_lo = (partial_rank - rank_top).astype(jnp.bfloat16)

    half = tokens // cores
    mine_q = jnp.concatenate([rows_q, rank_hi, rank_lo], axis=1)
    mine_q = lax.dynamic_slice_in_dim(mine_q, core * half, half, 0)
    expert_size = lax.axis_size("expert")
    arrived = lax.all_gather(mine_q, "expert", axis=1, tiled=False)
    swap = [(i, (i + 1) % cores) for i in range(cores)]
    halves = (arrived, lax.ppermute(arrived, "wc", swap))

    def true_order(mine, other):
        return jnp.where(
            core == 0, jnp.concatenate([mine, other], axis=0), jnp.concatenate([other, mine], axis=0)
        )

    def local_halves(whole):
        return tuple(
            lax.dynamic_slice_in_dim(whole, start * half, half, 0) for start in (core, 1 - core)
        )

    rows = []
    ranks = []
    for piece in halves:
        rows.append(piece[:, :, :quarter].reshape(half, expert_size * quarter))
        parts = piece[:, :, quarter:].astype(jnp.float32)
        ranks.append(
            jnp.sum(parts[:, :, : window * rank] + parts[:, :, window * rank :], axis=1).astype(
                jnp.bfloat16
            )
        )
    tile_up = jnp.take(adapter_up_weight, tile_tenant_index, axis=0)
    experts = jnp.arange(router.shape[1], dtype=jnp.int32)
    index_halves = local_halves(row_expert_index)
    weights = []
    adapted = []
    for h in range(2):
        logits = jnp.dot(rows[h], router, preferred_element_type=jnp.float32)
        picked = (index_halves[h][:, :, None] == experts[None, None, :]).astype(jnp.float32)
        chosen = jnp.sum(picked * logits[:, None, :], axis=2)
        first_prob = jax.nn.sigmoid(chosen[:, 0] - chosen[:, 1])
        second_prob = jax.nn.sigmoid(chosen[:, 1] - chosen[:, 0])
        weights.append(
            first_prob[:, None] * picked[:, 0, :window]
            + second_prob[:, None] * picked[:, 1, :window]
        )
        blank = jnp.zeros_like(ranks[h])
        placed = true_order(ranks[h], blank) if h == 0 else true_order(blank, ranks[h])
        adapted_all = jnp.einsum(
            "nter,nerf->ntef",
            placed.reshape(tile_count, tile_rows, window, rank),
            tile_up,
            preferred_element_type=jnp.float32,
        ).reshape(tokens, window, tile_up.shape[3])
        adapted.append(local_halves(adapted_all)[h])

    running = [None, None]
    previous = None
    for expert_number in range(window):
        hidden = []
        for h in range(2):
            gate_pre = jnp.dot(
                rows[h], gate_weight[expert_number], preferred_element_type=jnp.float32
            )
            up_value = (
                jnp.dot(rows[h], up_weight[expert_number], preferred_element_type=jnp.float32)
                + ADAPTER_SCALE * adapted[h][:, expert_number]
            )
            hidden.append(
                (weights[h][:, expert_number, None] * jax.nn.silu(gate_pre) * up_value).astype(
                    jnp.bfloat16
                )
            )
        if expert_number == 0:
            parts = []
            for hd in hidden:
                if previous is not None:
                    hd, _ = lax.optimization_barrier((hd, previous))
                previous = lax.all_gather(hd, "expert", axis=1, tiled=True)
                parts.append(
                    jnp.dot(previous, down_weight[expert_number], preferred_element_type=jnp.float32)
                )
        else:
            joined = jnp.concatenate(hidden, axis=0)
            joined, _ = lax.optimization_barrier((joined, previous))
            previous = lax.all_gather(joined, "expert", axis=1, tiled=True)
            part = jnp.dot(previous, down_weight[expert_number], preferred_element_type=jnp.float32)
            parts = [part[:half], part[half:]]
        running = [p if r is None else r + p for r, p in zip(running, parts)]
    return reduce_rows(true_order(*running), core, cores).astype(jnp.bfloat16)


def reduce_rows(running, core, cores):
    chips = lax.axis_size("wy")
    block = running.shape[0] // (chips * cores)
    by_chip = running.reshape(chips, cores, block, running.shape[1])
    keep = jnp.where(core == 0, by_chip[:, 0], by_chip[:, 1])
    send = jnp.where(core == 0, by_chip[:, 1], by_chip[:, 0])
    chip_sum = keep + lax.ppermute(send, "wc", [(i, (i + 1) % cores) for i in range(cores)])
    if chips == 2:
        chip = lax.axis_index("wy")
        mine = jnp.where(chip == 0, chip_sum[0], chip_sum[1])
        away = jnp.where(chip == 0, chip_sum[1], chip_sum[0])
        return mine + lax.ppermute(away, "wy", [(0, 1), (1, 0)])
    return lax.psum_scatter(chip_sum, "wy", scatter_dimension=0, tiled=True).reshape(block, -1)


def solution(mesh):
    groups = mesh.shape["groups"]
    wide = mesh.shape["wide"]
    expert = mesh.shape["expert"]
    split = Mesh(
        np.asarray(mesh.devices).reshape(groups, wide // 2, 2, expert),
        ("groups", "wy", "wc", "expert"),
    )
    rows = ("groups", "wy", "wc")
    in_specs = (
        P(rows, None, "expert"),
        P("groups"),
        P("groups", None),
        P("groups"),
        P("groups"),
        P(),
        P(None, None, GROUP),
        P(None, None, GROUP),
        P(None, WIDE, "expert"),
        P(rows, None, "expert", None),
        P("groups", None, None, GROUP),
    )
    out_specs = P(rows, "expert")
    return jax.shard_map(
        per_device, mesh=split, in_specs=in_specs, out_specs=out_specs, check_vma=False
    )
```

```python
import jax
import jax.numpy as jnp
import numpy as np
from jax import lax
from jax.sharding import Mesh
from jax.sharding import PartitionSpec as P

ADAPTER_SCALE = 0.5

WIDE = ("wy", "wc")
GROUP = ("wy", "wc", "expert")


def per_device(
    prompts,
    span_slot_owner,
    row_expert_index,
    tile_tenant_index,
    tenant_adapter_slot,
    router,
    gate_weight,
    up_weight,
    down_weight,
    adapter_down_weight,
    adapter_up_weight,
):
    span = prompts.shape[1]
    quarter = prompts.shape[2]
    tokens = row_expert_index.shape[0]
    nchunk = tokens // span
    window = gate_weight.shape[0]
    core = lax.axis_index("wc")
    cores = lax.axis_size("wc")
    wide_index = lax.axis_index(WIDE)

    tile_count = tile_tenant_index.shape[0]
    tile_rows = tokens // tile_count
    resident_slots = adapter_down_weight.shape[0]
    rank = adapter_down_weight.shape[3]
    slots_q = lax.all_gather(prompts, WIDE, axis=0, tiled=True)
    slot_of_span = span_slot_owner[:nchunk]
    rows_q = jnp.take(slots_q, slot_of_span, axis=0).reshape(tokens, quarter)

    chips = lax.axis_size("wy")
    tile_slot_index = jnp.take(tenant_adapter_slot, tile_tenant_index)
    holder = tile_slot_index // resident_slots
    local_slot = tile_slot_index % resident_slots
    if chips == 2 and cores == 2:
        swap = [(0, 1), (1, 0)]
        from_chip = lax.ppermute(adapter_down_weight, "wy", swap)
        from_core = lax.ppermute(adapter_down_weight, "wc", swap)
        from_both = lax.ppermute(from_chip, "wc", swap)
        stacked = jnp.stack([adapter_down_weight, from_core, from_chip, from_both])
        source = jnp.bitwise_xor(holder, wide_index)
    else:
        stacked = lax.all_gather(adapter_down_weight, WIDE, axis=0, tiled=False)
        source = holder
    flat_held = stacked.reshape((-1,) + adapter_down_weight.shape[1:])
    tile_adapters = jnp.take(flat_held, source * resident_slots + local_slot, axis=0)

    partial_rank = jnp.einsum(
        "ntd,nedr->nter",
        rows_q.reshape(tile_count, tile_rows, quarter),
        tile_adapters,
        preferred_element_type=jnp.float32,
    ).reshape(tokens, window * rank)
    rank_top = lax.reduce_precision(partial_rank, exponent_bits=8, mantissa_bits=7)
    rank_hi = rank_top.astype(jnp.bfloat16)
    rank_lo = (partial_rank - rank_top).astype(jnp.bfloat16)

    half = tokens // cores
    expert_size = lax.axis_size("expert")
    swap = [(i, (i + 1) % cores) for i in range(cores)]
    mine_q = lax.dynamic_slice_in_dim(rows_q, core * half, half, 0)
    mine = lax.all_gather(mine_q, "expert", axis=1, tiled=True)
    rank_q = lax.dynamic_slice_in_dim(
        jnp.concatenate([rank_hi, rank_lo], axis=1), core * half, half, 0
    )
    rank_q, _ = lax.optimization_barrier((rank_q, mine))
    pieces = lax.all_gather(rank_q, "expert", axis=1, tiled=False).astype(jnp.float32)
    mine_rank = jnp.sum(pieces[:, :, : window * rank] + pieces[:, :, window * rank :], axis=1)
    mine_rank = mine_rank.astype(jnp.bfloat16)
    other = lax.ppermute(mine, "wc", swap)
    other_rank = lax.ppermute(mine_rank, "wc", swap)
    input_rows = jnp.where(
        core == 0, jnp.concatenate([mine, other], axis=0), jnp.concatenate([other, mine], axis=0)
    )
    lowrank = jnp.where(
        core == 0,
        jnp.concatenate([mine_rank, other_rank], axis=0),
        jnp.concatenate([other_rank, mine_rank], axis=0),
    ).reshape(tile_count, tile_rows, window, rank)

    logits = jnp.dot(input_rows, router, preferred_element_type=jnp.float32)
    experts = jnp.arange(router.shape[1], dtype=jnp.int32)
    picked = (row_expert_index[:, :, None] == experts[None, None, :]).astype(jnp.float32)
    chosen = jnp.sum(picked * logits[:, None, :], axis=2)
    first_prob = jax.nn.sigmoid(chosen[:, 0] - chosen[:, 1])
    second_prob = jax.nn.sigmoid(chosen[:, 1] - chosen[:, 0])
    weight = (
        first_prob[:, None] * picked[:, 0, :window] + second_prob[:, None] * picked[:, 1, :window]
    )

    tile_up = jnp.take(adapter_up_weight, tile_tenant_index, axis=0)
    adapted_hidden = jnp.einsum(
        "nter,nerf->ntef", lowrank, tile_up, preferred_element_type=jnp.float32
    ).reshape(tokens, window, tile_up.shape[3])

    running = None
    for expert_number in range(window):
        gate_pre = jnp.dot(
            input_rows, gate_weight[expert_number], preferred_element_type=jnp.float32
        )
        up_value = (
            jnp.dot(input_rows, up_weight[expert_number], preferred_element_type=jnp.float32)
            + ADAPTER_SCALE * adapted_hidden[:, expert_number]
        )
        hidden = (
            weight[:, expert_number, None] * jax.nn.silu(gate_pre) * up_value
        ).astype(jnp.bfloat16)
        gathered = lax.all_gather(hidden, "expert", axis=1, tiled=True)
        part = jnp.dot(gathered, down_weight[expert_number], preferred_element_type=jnp.float32)
        running = part if running is None else running + part
    return reduce_rows(running, core, cores).astype(jnp.bfloat16)


def reduce_rows(running, core, cores):
    chips = lax.axis_size("wy")
    block = running.shape[0] // (chips * cores)
    by_chip = running.reshape(chips, cores, block, running.shape[1])
    keep = jnp.where(core == 0, by_chip[:, 0], by_chip[:, 1])
    send = jnp.where(core == 0, by_chip[:, 1], by_chip[:, 0])
    chip_sum = keep + lax.ppermute(send, "wc", [(i, (i + 1) % cores) for i in range(cores)])
    if chips == 2:
        chip = lax.axis_index("wy")
        mine = jnp.where(chip == 0, chip_sum[0], chip_sum[1])
        away = jnp.where(chip == 0, chip_sum[1], chip_sum[0])
        return mine + lax.ppermute(away, "wy", [(0, 1), (1, 0)])
    return lax.psum_scatter(chip_sum, "wy", scatter_dimension=0, tiled=True).reshape(block, -1)


def solution(mesh):
    groups = mesh.shape["groups"]
    wide = mesh.shape["wide"]
    expert = mesh.shape["expert"]
    split = Mesh(
        np.asarray(mesh.devices).reshape(groups, wide // 2, 2, expert),
        ("groups", "wy", "wc", "expert"),
    )
    rows = ("groups", "wy", "wc")
    in_specs = (
        P(rows, None, "expert"),
        P("groups"),
        P("groups", None),
        P("groups"),
        P("groups"),
        P(),
        P(None, None, GROUP),
        P(None, None, GROUP),
        P(None, WIDE, "expert"),
        P(rows, None, "expert", None),
        P("groups", None, None, GROUP),
    )
    out_specs = P(rows, "expert")
    return jax.shard_map(
        per_device, mesh=split, in_specs=in_specs, out_specs=out_specs, check_vma=False
    )
```

```python
import jax
import jax.numpy as jnp
import numpy as np
from jax import lax
from jax.sharding import Mesh
from jax.sharding import PartitionSpec as P

ADAPTER_SCALE = 0.5

WIDE = ("wy", "wc")
GROUP = ("wy", "wc", "expert")


def per_device(
    prompts,
    span_slot_owner,
    row_expert_index,
    tile_tenant_index,
    tenant_adapter_slot,
    router,
    gate_weight,
    up_weight,
    down_weight,
    adapter_down_weight,
    adapter_up_weight,
):
    span = prompts.shape[1]
    quarter = prompts.shape[2]
    tokens = row_expert_index.shape[0]
    nchunk = tokens // span
    window = gate_weight.shape[0]
    core = lax.axis_index("wc")
    cores = lax.axis_size("wc")
    wide_index = lax.axis_index(WIDE)

    tile_count = tile_tenant_index.shape[0]
    tile_rows = tokens // tile_count
    resident_slots = adapter_down_weight.shape[0]
    rank = adapter_down_weight.shape[3]
    slots_q = lax.all_gather(prompts, WIDE, axis=0, tiled=True)
    slot_of_span = span_slot_owner[:nchunk]
    rows_q = jnp.take(slots_q, slot_of_span, axis=0).reshape(tokens, quarter)

    chips = lax.axis_size("wy")
    tile_slot_index = jnp.take(tenant_adapter_slot, tile_tenant_index)
    holder = tile_slot_index // resident_slots
    local_slot = tile_slot_index % resident_slots
    if chips == 2 and cores == 2:
        swap = [(0, 1), (1, 0)]
        from_chip = lax.ppermute(adapter_down_weight, "wy", swap)
        from_core = lax.ppermute(adapter_down_weight, "wc", swap)
        from_both = lax.ppermute(from_chip, "wc", swap)
        stacked = jnp.stack([adapter_down_weight, from_core, from_chip, from_both])
        source = jnp.bitwise_xor(holder, wide_index)
    else:
        stacked = lax.all_gather(adapter_down_weight, WIDE, axis=0, tiled=False)
        source = holder
    flat_held = stacked.reshape((-1,) + adapter_down_weight.shape[1:])
    tile_adapters = jnp.take(flat_held, source * resident_slots + local_slot, axis=0)

    partial_rank = jnp.einsum(
        "ntd,nedr->nter",
        rows_q.reshape(tile_count, tile_rows, quarter),
        tile_adapters,
        preferred_element_type=jnp.float32,
    ).reshape(tokens, window * rank)
    rank_top = lax.reduce_precision(partial_rank, exponent_bits=8, mantissa_bits=7)
    rank_hi = rank_top.astype(jnp.bfloat16)
    rank_lo = (partial_rank - rank_top).astype(jnp.bfloat16)

    half = tokens // cores
    expert_size = lax.axis_size("expert")
    swap = [(i, (i + 1) % cores) for i in range(cores)]
    mine_q = lax.dynamic_slice_in_dim(rows_q, core * half, half, 0)
    mine = lax.all_gather(mine_q, "expert", axis=1, tiled=True)
    rank_q = lax.dynamic_slice_in_dim(
        jnp.concatenate([rank_hi, rank_lo], axis=1), core * half, half, 0
    )
    rank_q, _ = lax.optimization_barrier((rank_q, mine))
    arrivals = [rank_q] + [
        lax.ppermute(rank_q, "expert", [(i, (i + shift) % expert_size) for i in range(expert_size)])
        for shift in range(1, expert_size)
    ]
    mine_rank = None
    for piece in arrivals:
        piece = piece.astype(jnp.float32)
        piece = piece[:, : window * rank] + piece[:, window * rank :]
        mine_rank = piece if mine_rank is None else mine_rank + piece
    mine_rank = mine_rank.astype(jnp.bfloat16)
    other = lax.ppermute(mine, "wc", swap)
    other_rank = lax.ppermute(mine_rank, "wc", swap)
    input_rows = jnp.where(
        core == 0, jnp.concatenate([mine, other], axis=0), jnp.concatenate([other, mine], axis=0)
    )
    lowrank = jnp.where(
        core == 0,
        jnp.concatenate([mine_rank, other_rank], axis=0),
        jnp.concatenate([other_rank, mine_rank], axis=0),
    ).reshape(tile_count, tile_rows, window, rank)

    logits = jnp.dot(input_rows, router, preferred_element_type=jnp.float32)
    experts = jnp.arange(router.shape[1], dtype=jnp.int32)
    picked = (row_expert_index[:, :, None] == experts[None, None, :]).astype(jnp.float32)
    chosen = jnp.sum(picked * logits[:, None, :], axis=2)
    first_prob = jax.nn.sigmoid(chosen[:, 0] - chosen[:, 1])
    second_prob = jax.nn.sigmoid(chosen[:, 1] - chosen[:, 0])
    weight = (
        first_prob[:, None] * picked[:, 0, :window] + second_prob[:, None] * picked[:, 1, :window]
    )

    tile_up = jnp.take(adapter_up_weight, tile_tenant_index, axis=0)
    adapted_hidden = jnp.einsum(
        "nter,nerf->ntef", lowrank, tile_up, preferred_element_type=jnp.float32
    ).reshape(tokens, window, tile_up.shape[3])

    running = None
    for expert_number in range(window):
        gate_pre = jnp.dot(
            input_rows, gate_weight[expert_number], preferred_element_type=jnp.float32
        )
        up_value = (
            jnp.dot(input_rows, up_weight[expert_number], preferred_element_type=jnp.float32)
            + ADAPTER_SCALE * adapted_hidden[:, expert_number]
        )
        hidden = (
            weight[:, expert_number, None] * jax.nn.silu(gate_pre) * up_value
        ).astype(jnp.bfloat16)
        gathered = lax.all_gather(hidden, "expert", axis=1, tiled=True)
        part = jnp.dot(gathered, down_weight[expert_number], preferred_element_type=jnp.float32)
        running = part if running is None else running + part
    return reduce_rows(running, core, cores).astype(jnp.bfloat16)


def reduce_rows(running, core, cores):
    chips = lax.axis_size("wy")
    block = running.shape[0] // (chips * cores)
    by_chip = running.reshape(chips, cores, block, running.shape[1])
    keep = jnp.where(core == 0, by_chip[:, 0], by_chip[:, 1])
    send = jnp.where(core == 0, by_chip[:, 1], by_chip[:, 0])
    chip_sum = keep + lax.ppermute(send, "wc", [(i, (i + 1) % cores) for i in range(cores)])
    if chips == 2:
        chip = lax.axis_index("wy")
        mine = jnp.where(chip == 0, chip_sum[0], chip_sum[1])
        away = jnp.where(chip == 0, chip_sum[1], chip_sum[0])
        return mine + lax.ppermute(away, "wy", [(0, 1), (1, 0)])
    return lax.psum_scatter(chip_sum, "wy", scatter_dimension=0, tiled=True).reshape(block, -1)


def solution(mesh):
    groups = mesh.shape["groups"]
    wide = mesh.shape["wide"]
    expert = mesh.shape["expert"]
    split = Mesh(
        np.asarray(mesh.devices).reshape(groups, wide // 2, 2, expert),
        ("groups", "wy", "wc", "expert"),
    )
    rows = ("groups", "wy", "wc")
    in_specs = (
        P(rows, None, "expert"),
        P("groups"),
        P("groups", None),
        P("groups"),
        P("groups"),
        P(),
        P(None, None, GROUP),
        P(None, None, GROUP),
        P(None, WIDE, "expert"),
        P(rows, None, "expert", None),
        P("groups", None, None, GROUP),
    )
    out_specs = P(rows, "expert")
    return jax.shard_map(
        per_device, mesh=split, in_specs=in_specs, out_specs=out_specs, check_vma=False
    )
```

```python
import jax
import jax.numpy as jnp
import numpy as np
from jax import lax
from jax.sharding import Mesh
from jax.sharding import PartitionSpec as P

ADAPTER_SCALE = 0.5

WIDE = ("wy", "wc")
GROUP = ("wy", "wc", "expert")


def per_device(
    prompts,
    span_slot_owner,
    row_expert_index,
    tile_tenant_index,
    tenant_adapter_slot,
    router,
    gate_weight,
    up_weight,
    down_weight,
    adapter_down_weight,
    adapter_up_weight,
):
    span = prompts.shape[1]
    quarter = prompts.shape[2]
    tokens = row_expert_index.shape[0]
    nchunk = tokens // span
    window = gate_weight.shape[0]
    core = lax.axis_index("wc")
    cores = lax.axis_size("wc")
    wide_index = lax.axis_index(WIDE)

    tile_count = tile_tenant_index.shape[0]
    tile_rows = tokens // tile_count
    resident_slots = adapter_down_weight.shape[0]
    rank = adapter_down_weight.shape[3]
    slots_q = lax.all_gather(prompts, WIDE, axis=0, tiled=True)
    slot_of_span = span_slot_owner[:nchunk]
    rows_q = jnp.take(slots_q, slot_of_span, axis=0).reshape(tokens, quarter)

    chips = lax.axis_size("wy")
    tile_slot_index = jnp.take(tenant_adapter_slot, tile_tenant_index)
    holder = tile_slot_index // resident_slots
    local_slot = tile_slot_index % resident_slots
    if chips == 2 and cores == 2:
        swap = [(0, 1), (1, 0)]
        from_chip = lax.ppermute(adapter_down_weight, "wy", swap)
        from_core = lax.ppermute(adapter_down_weight, "wc", swap)
        from_both = lax.ppermute(from_chip, "wc", swap)
        stacked = jnp.stack([adapter_down_weight, from_core, from_chip, from_both])
        source = jnp.bitwise_xor(holder, wide_index)
    else:
        stacked = lax.all_gather(adapter_down_weight, WIDE, axis=0, tiled=False)
        source = holder
    flat_held = stacked.reshape((-1,) + adapter_down_weight.shape[1:])
    tile_adapters = jnp.take(flat_held, source * resident_slots + local_slot, axis=0)

    partial_rank = jnp.einsum(
        "ntd,nedr->nter",
        rows_q.reshape(tile_count, tile_rows, quarter),
        tile_adapters,
        preferred_element_type=jnp.float32,
    ).reshape(tokens, window * rank)
    rank_top = lax.reduce_precision(partial_rank, exponent_bits=8, mantissa_bits=7)
    rank_hi = rank_top.astype(jnp.bfloat16)
    rank_lo = (partial_rank - rank_top).astype(jnp.bfloat16)

    half = tokens // cores
    expert_size = lax.axis_size("expert")
    swap = [(i, (i + 1) % cores) for i in range(cores)]
    mine_q = lax.dynamic_slice_in_dim(rows_q, core * half, half, 0)
    mine = lax.all_gather(mine_q, "expert", axis=1, tiled=True)
    rank_q = lax.dynamic_slice_in_dim(
        jnp.concatenate([rank_hi, rank_lo], axis=1), core * half, half, 0
    )
    rank_q, _ = lax.optimization_barrier((rank_q, mine))
    pieces = lax.all_gather(rank_q, "expert", axis=1, tiled=False).astype(jnp.float32)
    mine_rank = jnp.sum(pieces[:, :, : window * rank] + pieces[:, :, window * rank :], axis=1)
    mine_rank = mine_rank.astype(jnp.bfloat16)
    other = lax.ppermute(mine, "wc", swap)
    other_rank = lax.ppermute(mine_rank, "wc", swap)
    input_rows = jnp.where(
        core == 0, jnp.concatenate([mine, other], axis=0), jnp.concatenate([other, mine], axis=0)
    )
    input_rows = lax.optimization_barrier(input_rows)
    lowrank = jnp.where(
        core == 0,
        jnp.concatenate([mine_rank, other_rank], axis=0),
        jnp.concatenate([other_rank, mine_rank], axis=0),
    ).reshape(tile_count, tile_rows, window, rank)

    logits = jnp.dot(input_rows, router, preferred_element_type=jnp.float32)
    experts = jnp.arange(router.shape[1], dtype=jnp.int32)
    picked = (row_expert_index[:, :, None] == experts[None, None, :]).astype(jnp.float32)
    chosen = jnp.sum(picked * logits[:, None, :], axis=2)
    first_prob = jax.nn.sigmoid(chosen[:, 0] - chosen[:, 1])
    second_prob = jax.nn.sigmoid(chosen[:, 1] - chosen[:, 0])
    weight = (
        first_prob[:, None] * picked[:, 0, :window] + second_prob[:, None] * picked[:, 1, :window]
    )

    tile_up = jnp.take(adapter_up_weight, tile_tenant_index, axis=0)
    adapted_hidden = jnp.einsum(
        "nter,nerf->ntef", lowrank, tile_up, preferred_element_type=jnp.float32
    ).reshape(tokens, window, tile_up.shape[3])

    running = None
    for expert_number in range(window):
        gate_pre = jnp.dot(
            input_rows, gate_weight[expert_number], preferred_element_type=jnp.float32
        )
        up_value = (
            jnp.dot(input_rows, up_weight[expert_number], preferred_element_type=jnp.float32)
            + ADAPTER_SCALE * adapted_hidden[:, expert_number]
        )
        hidden = (
            weight[:, expert_number, None] * jax.nn.silu(gate_pre) * up_value
        ).astype(jnp.bfloat16)
        gathered = lax.all_gather(hidden, "expert", axis=1, tiled=True)
        part = jnp.dot(gathered, down_weight[expert_number], preferred_element_type=jnp.float32)
        running = part if running is None else running + part
    return reduce_rows(running, core, cores).astype(jnp.bfloat16)


def reduce_rows(running, core, cores):
    chips = lax.axis_size("wy")
    block = running.shape[0] // (chips * cores)
    by_chip = running.reshape(chips, cores, block, running.shape[1])
    keep = jnp.where(core == 0, by_chip[:, 0], by_chip[:, 1])
    send = jnp.where(core == 0, by_chip[:, 1], by_chip[:, 0])
    chip_sum = keep + lax.ppermute(send, "wc", [(i, (i + 1) % cores) for i in range(cores)])
    if chips == 2:
        chip = lax.axis_index("wy")
        mine = jnp.where(chip == 0, chip_sum[0], chip_sum[1])
        away = jnp.where(chip == 0, chip_sum[1], chip_sum[0])
        return mine + lax.ppermute(away, "wy", [(0, 1), (1, 0)])
    return lax.psum_scatter(chip_sum, "wy", scatter_dimension=0, tiled=True).reshape(block, -1)


def solution(mesh):
    groups = mesh.shape["groups"]
    wide = mesh.shape["wide"]
    expert = mesh.shape["expert"]
    split = Mesh(
        np.asarray(mesh.devices).reshape(groups, wide // 2, 2, expert),
        ("groups", "wy", "wc", "expert"),
    )
    rows = ("groups", "wy", "wc")
    in_specs = (
        P(rows, None, "expert"),
        P("groups"),
        P("groups", None),
        P("groups"),
        P("groups"),
        P(),
        P(None, None, GROUP),
        P(None, None, GROUP),
        P(None, WIDE, "expert"),
        P(rows, None, "expert", None),
        P("groups", None, None, GROUP),
    )
    out_specs = P(rows, "expert")
    return jax.shard_map(
        per_device, mesh=split, in_specs=in_specs, out_specs=out_specs, check_vma=False
    )
```

```python
import jax
import jax.numpy as jnp
import numpy as np
from jax import lax
from jax.sharding import Mesh
from jax.sharding import PartitionSpec as P

ADAPTER_SCALE = 0.5

WIDE = ("wy", "wc")
GROUP = ("wy", "wc", "expert")


def per_device(
    prompts,
    span_slot_owner,
    row_expert_index,
    tile_tenant_index,
    tenant_adapter_slot,
    router,
    gate_weight,
    up_weight,
    down_weight,
    adapter_down_weight,
    adapter_up_weight,
):
    span = prompts.shape[1]
    quarter = prompts.shape[2]
    tokens = row_expert_index.shape[0]
    nchunk = tokens // span
    window = gate_weight.shape[0]
    core = lax.axis_index("wc")
    cores = lax.axis_size("wc")
    wide_index = lax.axis_index(WIDE)

    tile_count = tile_tenant_index.shape[0]
    tile_rows = tokens // tile_count
    resident_slots = adapter_down_weight.shape[0]
    rank = adapter_down_weight.shape[3]
    slots_q = lax.all_gather(prompts, WIDE, axis=0, tiled=True)
    slot_of_span = span_slot_owner[:nchunk]
    rows_q = jnp.take(slots_q, slot_of_span, axis=0).reshape(tokens, quarter)

    chips = lax.axis_size("wy")
    tile_slot_index = jnp.take(tenant_adapter_slot, tile_tenant_index)
    holder = tile_slot_index // resident_slots
    local_slot = tile_slot_index % resident_slots
    if chips == 2 and cores == 2:
        swap = [(0, 1), (1, 0)]
        from_chip = lax.ppermute(adapter_down_weight, "wy", swap)
        from_core = lax.ppermute(adapter_down_weight, "wc", swap)
        from_both = lax.ppermute(from_chip, "wc", swap)
        stacked = jnp.stack([adapter_down_weight, from_core, from_chip, from_both])
        source = jnp.bitwise_xor(holder, wide_index)
    else:
        stacked = lax.all_gather(adapter_down_weight, WIDE, axis=0, tiled=False)
        source = holder
    flat_held = stacked.reshape((-1,) + adapter_down_weight.shape[1:])
    tile_adapters = jnp.take(flat_held, source * resident_slots + local_slot, axis=0)

    partial_rank = jnp.einsum(
        "ntd,nedr->nter",
        rows_q.reshape(tile_count, tile_rows, quarter),
        tile_adapters,
        preferred_element_type=jnp.float32,
    ).reshape(tokens, window * rank)
    rank_top = lax.reduce_precision(partial_rank, exponent_bits=8, mantissa_bits=7)
    rank_hi = rank_top.astype(jnp.bfloat16)
    rank_lo = (partial_rank - rank_top).astype(jnp.bfloat16)

    half = tokens // cores
    expert_size = lax.axis_size("expert")
    swap = [(i, (i + 1) % cores) for i in range(cores)]
    mine_q = lax.dynamic_slice_in_dim(rows_q, core * half, half, 0)
    mine = lax.all_gather(mine_q, "expert", axis=1, tiled=True)
    rank_q = lax.dynamic_slice_in_dim(
        jnp.concatenate([rank_hi, rank_lo], axis=1), core * half, half, 0
    )
    rank_q, _ = lax.optimization_barrier((rank_q, mine))
    pieces = lax.all_gather(rank_q, "expert", axis=1, tiled=False).astype(jnp.float32)
    mine_rank = jnp.sum(pieces[:, :, : window * rank] + pieces[:, :, window * rank :], axis=1)
    mine_rank = mine_rank.astype(jnp.bfloat16)
    other = lax.ppermute(mine, "wc", swap)
    other_rank = lax.ppermute(mine_rank, "wc", swap)
    input_rows = jnp.where(
        core == 0, jnp.concatenate([mine, other], axis=0), jnp.concatenate([other, mine], axis=0)
    )
    input_rows = lax.optimization_barrier(input_rows)
    lowrank = jnp.where(
        core == 0,
        jnp.concatenate([mine_rank, other_rank], axis=0),
        jnp.concatenate([other_rank, mine_rank], axis=0),
    ).reshape(tile_count, tile_rows, window, rank)

    logits = jnp.dot(input_rows, router, preferred_element_type=jnp.float32)
    experts = jnp.arange(router.shape[1], dtype=jnp.int32)
    picked = (row_expert_index[:, :, None] == experts[None, None, :]).astype(jnp.float32)
    chosen = jnp.sum(picked * logits[:, None, :], axis=2)
    first_prob = jax.nn.sigmoid(chosen[:, 0] - chosen[:, 1])
    second_prob = jax.nn.sigmoid(chosen[:, 1] - chosen[:, 0])
    weight = (
        first_prob[:, None] * picked[:, 0, :window] + second_prob[:, None] * picked[:, 1, :window]
    )

    tile_up = jnp.take(adapter_up_weight, tile_tenant_index, axis=0)
    adapted_hidden = jnp.einsum(
        "nter,nerf->ntef", lowrank, tile_up, preferred_element_type=jnp.float32
    ).reshape(tokens, window, tile_up.shape[3])

    running = None
    for expert_number in range(window):
        gate_pre = jnp.dot(
            input_rows, gate_weight[expert_number], preferred_element_type=jnp.float32
        )
        up_value = (
            jnp.dot(input_rows, up_weight[expert_number], preferred_element_type=jnp.float32)
            + ADAPTER_SCALE * adapted_hidden[:, expert_number]
        )
        hidden = (
            weight[:, expert_number, None] * jax.nn.silu(gate_pre) * up_value
        ).astype(jnp.bfloat16)
        gathered = lax.all_gather(hidden, "expert", axis=1, tiled=True)
        if expert_number < window - 1:
            part = jnp.dot(gathered, down_weight[expert_number], preferred_element_type=jnp.float32)
            running = part if running is None else running + part
            continue
        width = down_weight.shape[2] // 2
        outs = []
        for c in range(2):
            cols = slice(c * width, (c + 1) * width)
            part = jnp.dot(
                gathered, down_weight[expert_number, :, cols], preferred_element_type=jnp.float32
            )
            if running is not None:
                part = running[:, cols] + part
            outs.append(reduce_rows(part, core, cores))
    return jnp.concatenate(outs, axis=1).astype(jnp.bfloat16)


def reduce_rows(running, core, cores):
    chips = lax.axis_size("wy")
    block = running.shape[0] // (chips * cores)
    by_chip = running.reshape(chips, cores, block, running.shape[1])
    keep = jnp.where(core == 0, by_chip[:, 0], by_chip[:, 1])
    send = jnp.where(core == 0, by_chip[:, 1], by_chip[:, 0])
    chip_sum = keep + lax.ppermute(send, "wc", [(i, (i + 1) % cores) for i in range(cores)])
    if chips == 2:
        chip = lax.axis_index("wy")
        mine = jnp.where(chip == 0, chip_sum[0], chip_sum[1])
        away = jnp.where(chip == 0, chip_sum[1], chip_sum[0])
        return mine + lax.ppermute(away, "wy", [(0, 1), (1, 0)])
    return lax.psum_scatter(chip_sum, "wy", scatter_dimension=0, tiled=True).reshape(block, -1)


def solution(mesh):
    groups = mesh.shape["groups"]
    wide = mesh.shape["wide"]
    expert = mesh.shape["expert"]
    split = Mesh(
        np.asarray(mesh.devices).reshape(groups, wide // 2, 2, expert),
        ("groups", "wy", "wc", "expert"),
    )
    rows = ("groups", "wy", "wc")
    in_specs = (
        P(rows, None, "expert"),
        P("groups"),
        P("groups", None),
        P("groups"),
        P("groups"),
        P(),
        P(None, None, GROUP),
        P(None, None, GROUP),
        P(None, WIDE, "expert"),
        P(rows, None, "expert", None),
        P("groups", None, None, GROUP),
    )
    out_specs = P(rows, "expert")
    return jax.shard_map(
        per_device, mesh=split, in_specs=in_specs, out_specs=out_specs, check_vma=False
    )
```

```python
import jax
import jax.numpy as jnp
import numpy as np
from jax import lax
from jax.sharding import Mesh
from jax.sharding import PartitionSpec as P

ADAPTER_SCALE = 0.5

WIDE = ("wy", "wc")
GROUP = ("wy", "wc", "expert")


def per_device(
    prompts,
    span_slot_owner,
    row_expert_index,
    tile_tenant_index,
    tenant_adapter_slot,
    router,
    gate_weight,
    up_weight,
    down_weight,
    adapter_down_weight,
    adapter_up_weight,
):
    span = prompts.shape[1]
    quarter = prompts.shape[2]
    tokens = row_expert_index.shape[0]
    nchunk = tokens // span
    window = gate_weight.shape[0]
    core = lax.axis_index("wc")
    cores = lax.axis_size("wc")
    wide_index = lax.axis_index(WIDE)

    tile_count = tile_tenant_index.shape[0]
    tile_rows = tokens // tile_count
    resident_slots = adapter_down_weight.shape[0]
    rank = adapter_down_weight.shape[3]
    slots_q = lax.all_gather(prompts, WIDE, axis=0, tiled=True)
    slot_of_span = span_slot_owner[:nchunk]
    rows_q = jnp.take(slots_q, slot_of_span, axis=0).reshape(tokens, quarter)

    chips = lax.axis_size("wy")
    tile_slot_index = jnp.take(tenant_adapter_slot, tile_tenant_index)
    holder = tile_slot_index // resident_slots
    local_slot = tile_slot_index % resident_slots
    if chips == 2 and cores == 2:
        swap = [(0, 1), (1, 0)]
        from_chip = lax.ppermute(adapter_down_weight, "wy", swap)
        from_core = lax.ppermute(adapter_down_weight, "wc", swap)
        from_both = lax.ppermute(from_chip, "wc", swap)
        stacked = jnp.stack([adapter_down_weight, from_core, from_chip, from_both])
        source = jnp.bitwise_xor(holder, wide_index)
    else:
        stacked = lax.all_gather(adapter_down_weight, WIDE, axis=0, tiled=False)
        source = holder
    flat_held = stacked.reshape((-1,) + adapter_down_weight.shape[1:])
    tile_adapters = jnp.take(flat_held, source * resident_slots + local_slot, axis=0)

    partial_rank = jnp.einsum(
        "ntd,nedr->nter",
        rows_q.reshape(tile_count, tile_rows, quarter),
        tile_adapters,
        preferred_element_type=jnp.float32,
    ).reshape(tokens, window * rank)
    rank_top = lax.reduce_precision(partial_rank, exponent_bits=8, mantissa_bits=7)
    rank_hi = rank_top.astype(jnp.bfloat16)
    rank_lo = (partial_rank - rank_top).astype(jnp.bfloat16)

    half = tokens // cores
    expert_size = lax.axis_size("expert")
    swap = [(i, (i + 1) % cores) for i in range(cores)]
    rank_q = lax.dynamic_slice_in_dim(
        jnp.concatenate([rank_hi, rank_lo], axis=1), core * half, half, 0
    )
    rank_rows = rank_q.reshape(-1, quarter)
    mine_q = jnp.concatenate(
        [lax.dynamic_slice_in_dim(rows_q, core * half, half, 0), rank_rows], axis=0
    )
    arrived = lax.all_gather(mine_q, "expert", axis=1, tiled=True)
    mine = arrived[:half]
    pieces = jnp.transpose(
        arrived[half:].reshape(rank_rows.shape[0], expert_size, quarter), (1, 0, 2)
    ).reshape(expert_size, half, rank_q.shape[1]).astype(jnp.float32)
    mine_rank = jnp.sum(pieces[:, :, : window * rank] + pieces[:, :, window * rank :], axis=0)
    mine_rank = mine_rank.astype(jnp.bfloat16)
    other = lax.ppermute(mine, "wc", swap)
    other_rank = lax.ppermute(mine_rank, "wc", swap)
    input_rows = jnp.where(
        core == 0, jnp.concatenate([mine, other], axis=0), jnp.concatenate([other, mine], axis=0)
    )
    input_rows = lax.optimization_barrier(input_rows)
    lowrank = jnp.where(
        core == 0,
        jnp.concatenate([mine_rank, other_rank], axis=0),
        jnp.concatenate([other_rank, mine_rank], axis=0),
    ).reshape(tile_count, tile_rows, window, rank)

    logits = jnp.dot(input_rows, router, preferred_element_type=jnp.float32)
    experts = jnp.arange(router.shape[1], dtype=jnp.int32)
    picked = (row_expert_index[:, :, None] == experts[None, None, :]).astype(jnp.float32)
    chosen = jnp.sum(picked * logits[:, None, :], axis=2)
    first_prob = jax.nn.sigmoid(chosen[:, 0] - chosen[:, 1])
    second_prob = jax.nn.sigmoid(chosen[:, 1] - chosen[:, 0])
    weight = (
        first_prob[:, None] * picked[:, 0, :window] + second_prob[:, None] * picked[:, 1, :window]
    )

    tile_up = jnp.take(adapter_up_weight, tile_tenant_index, axis=0)
    adapted_hidden = jnp.einsum(
        "nter,nerf->ntef", lowrank, tile_up, preferred_element_type=jnp.float32
    ).reshape(tokens, window, tile_up.shape[3])

    running = None
    for expert_number in range(window):
        gate_pre = jnp.dot(
            input_rows, gate_weight[expert_number], preferred_element_type=jnp.float32
        )
        up_value = (
            jnp.dot(input_rows, up_weight[expert_number], preferred_element_type=jnp.float32)
            + ADAPTER_SCALE * adapted_hidden[:, expert_number]
        )
        hidden = (
            weight[:, expert_number, None] * jax.nn.silu(gate_pre) * up_value
        ).astype(jnp.bfloat16)
        gathered = lax.all_gather(hidden, "expert", axis=1, tiled=True)
        part = jnp.dot(gathered, down_weight[expert_number], preferred_element_type=jnp.float32)
        running = part if running is None else running + part
    return reduce_rows(running, core, cores).astype(jnp.bfloat16)


def reduce_rows(running, core, cores):
    chips = lax.axis_size("wy")
    block = running.shape[0] // (chips * cores)
    by_chip = running.reshape(chips, cores, block, running.shape[1])
    keep = jnp.where(core == 0, by_chip[:, 0], by_chip[:, 1])
    send = jnp.where(core == 0, by_chip[:, 1], by_chip[:, 0])
    chip_sum = keep + lax.ppermute(send, "wc", [(i, (i + 1) % cores) for i in range(cores)])
    if chips == 2:
        chip = lax.axis_index("wy")
        mine = jnp.where(chip == 0, chip_sum[0], chip_sum[1])
        away = jnp.where(chip == 0, chip_sum[1], chip_sum[0])
        return mine + lax.ppermute(away, "wy", [(0, 1), (1, 0)])
    return lax.psum_scatter(chip_sum, "wy", scatter_dimension=0, tiled=True).reshape(block, -1)


def solution(mesh):
    groups = mesh.shape["groups"]
    wide = mesh.shape["wide"]
    expert = mesh.shape["expert"]
    split = Mesh(
        np.asarray(mesh.devices).reshape(groups, wide // 2, 2, expert),
        ("groups", "wy", "wc", "expert"),
    )
    rows = ("groups", "wy", "wc")
    in_specs = (
        P(rows, None, "expert"),
        P("groups"),
        P("groups", None),
        P("groups"),
        P("groups"),
        P(),
        P(None, None, GROUP),
        P(None, None, GROUP),
        P(None, WIDE, "expert"),
        P(rows, None, "expert", None),
        P("groups", None, None, GROUP),
    )
    out_specs = P(rows, "expert")
    return jax.shard_map(
        per_device, mesh=split, in_specs=in_specs, out_specs=out_specs, check_vma=False
    )
```

```python
import jax
import jax.numpy as jnp
import numpy as np
from jax import lax
from jax.sharding import Mesh
from jax.sharding import PartitionSpec as P

ADAPTER_SCALE = 0.5

WIDE = ("wy", "wc")
GROUP = ("wy", "wc", "expert")


def per_device(
    prompts,
    span_slot_owner,
    row_expert_index,
    tile_tenant_index,
    tenant_adapter_slot,
    router,
    gate_weight,
    up_weight,
    down_weight,
    adapter_down_weight,
    adapter_up_weight,
):
    span = prompts.shape[1]
    quarter = prompts.shape[2]
    tokens = row_expert_index.shape[0]
    nchunk = tokens // span
    window = gate_weight.shape[0]
    core = lax.axis_index("wc")
    cores = lax.axis_size("wc")
    wide_index = lax.axis_index(WIDE)

    tile_count = tile_tenant_index.shape[0]
    tile_rows = tokens // tile_count
    resident_slots = adapter_down_weight.shape[0]
    rank = adapter_down_weight.shape[3]
    slot_of_span = span_slot_owner[:nchunk]
    held_slots = prompts.shape[0]
    if lax.axis_size("wy") == 2 and cores == 2:
        pair = [(0, 1), (1, 0)]
        slot_chip = lax.ppermute(prompts, "wy", pair)
        slot_core = lax.ppermute(prompts, "wc", pair)
        slot_both = lax.ppermute(slot_chip, "wc", pair)
        slots_q = jnp.concatenate([prompts, slot_core, slot_chip, slot_both], axis=0)
        slot_pick = (
            jnp.bitwise_xor(slot_of_span // held_slots, wide_index) * held_slots
            + slot_of_span % held_slots
        )
    else:
        slots_q = lax.all_gather(prompts, WIDE, axis=0, tiled=True)
        slot_pick = slot_of_span
    rows_q = jnp.take(slots_q, slot_pick, axis=0).reshape(tokens, quarter)

    chips = lax.axis_size("wy")
    tile_slot_index = jnp.take(tenant_adapter_slot, tile_tenant_index)
    holder = tile_slot_index // resident_slots
    local_slot = tile_slot_index % resident_slots
    if chips == 2 and cores == 2:
        swap = [(0, 1), (1, 0)]
        from_chip = lax.ppermute(adapter_down_weight, "wy", swap)
        from_core = lax.ppermute(adapter_down_weight, "wc", swap)
        from_both = lax.ppermute(from_chip, "wc", swap)
        stacked = jnp.stack([adapter_down_weight, from_core, from_chip, from_both])
        source = jnp.bitwise_xor(holder, wide_index)
    else:
        stacked = lax.all_gather(adapter_down_weight, WIDE, axis=0, tiled=False)
        source = holder
    flat_held = stacked.reshape((-1,) + adapter_down_weight.shape[1:])
    tile_adapters = jnp.take(flat_held, source * resident_slots + local_slot, axis=0)

    partial_rank = jnp.einsum(
        "ntd,nedr->nter",
        rows_q.reshape(tile_count, tile_rows, quarter),
        tile_adapters,
        preferred_element_type=jnp.float32,
    ).reshape(tokens, window * rank)
    rank_top = lax.reduce_precision(partial_rank, exponent_bits=8, mantissa_bits=7)
    rank_hi = rank_top.astype(jnp.bfloat16)
    rank_lo = (partial_rank - rank_top).astype(jnp.bfloat16)

    half = tokens // cores
    expert_size = lax.axis_size("expert")
    swap = [(i, (i + 1) % cores) for i in range(cores)]
    mine_q = lax.dynamic_slice_in_dim(rows_q, core * half, half, 0)
    mine = lax.all_gather(mine_q, "expert", axis=1, tiled=True)
    rank_q = lax.dynamic_slice_in_dim(
        jnp.concatenate([rank_hi, rank_lo], axis=1), core * half, half, 0
    )
    rank_q, _ = lax.optimization_barrier((rank_q, mine))
    pieces = lax.all_gather(rank_q, "expert", axis=1, tiled=False).astype(jnp.float32)
    mine_rank = jnp.sum(pieces[:, :, : window * rank] + pieces[:, :, window * rank :], axis=1)
    mine_rank = mine_rank.astype(jnp.bfloat16)
    other = lax.ppermute(mine, "wc", swap)
    other_rank = lax.ppermute(mine_rank, "wc", swap)
    input_rows = jnp.where(
        core == 0, jnp.concatenate([mine, other], axis=0), jnp.concatenate([other, mine], axis=0)
    )
    input_rows = lax.optimization_barrier(input_rows)
    lowrank = jnp.where(
        core == 0,
        jnp.concatenate([mine_rank, other_rank], axis=0),
        jnp.concatenate([other_rank, mine_rank], axis=0),
    ).reshape(tile_count, tile_rows, window, rank)

    logits = jnp.dot(input_rows, router, preferred_element_type=jnp.float32)
    experts = jnp.arange(router.shape[1], dtype=jnp.int32)
    picked = (row_expert_index[:, :, None] == experts[None, None, :]).astype(jnp.float32)
    chosen = jnp.sum(picked * logits[:, None, :], axis=2)
    first_prob = jax.nn.sigmoid(chosen[:, 0] - chosen[:, 1])
    second_prob = jax.nn.sigmoid(chosen[:, 1] - chosen[:, 0])
    weight = (
        first_prob[:, None] * picked[:, 0, :window] + second_prob[:, None] * picked[:, 1, :window]
    )

    tile_up = jnp.take(adapter_up_weight, tile_tenant_index, axis=0)
    adapted_hidden = jnp.einsum(
        "nter,nerf->ntef", lowrank, tile_up, preferred_element_type=jnp.float32
    ).reshape(tokens, window, tile_up.shape[3])

    running = None
    for expert_number in range(window):
        gate_pre = jnp.dot(
            input_rows, gate_weight[expert_number], preferred_element_type=jnp.float32
        )
        up_value = (
            jnp.dot(input_rows, up_weight[expert_number], preferred_element_type=jnp.float32)
            + ADAPTER_SCALE * adapted_hidden[:, expert_number]
        )
        hidden = (
            weight[:, expert_number, None] * jax.nn.silu(gate_pre) * up_value
        ).astype(jnp.bfloat16)
        gathered = lax.all_gather(hidden, "expert", axis=1, tiled=True)
        part = jnp.dot(gathered, down_weight[expert_number], preferred_element_type=jnp.float32)
        running = part if running is None else running + part
    return reduce_rows(running, core, cores).astype(jnp.bfloat16)


def reduce_rows(running, core, cores):
    chips = lax.axis_size("wy")
    block = running.shape[0] // (chips * cores)
    by_chip = running.reshape(chips, cores, block, running.shape[1])
    keep = jnp.where(core == 0, by_chip[:, 0], by_chip[:, 1])
    send = jnp.where(core == 0, by_chip[:, 1], by_chip[:, 0])
    chip_sum = keep + lax.ppermute(send, "wc", [(i, (i + 1) % cores) for i in range(cores)])
    if chips == 2:
        chip = lax.axis_index("wy")
        mine = jnp.where(chip == 0, chip_sum[0], chip_sum[1])
        away = jnp.where(chip == 0, chip_sum[1], chip_sum[0])
        return mine + lax.ppermute(away, "wy", [(0, 1), (1, 0)])
    return lax.psum_scatter(chip_sum, "wy", scatter_dimension=0, tiled=True).reshape(block, -1)


def solution(mesh):
    groups = mesh.shape["groups"]
    wide = mesh.shape["wide"]
    expert = mesh.shape["expert"]
    split = Mesh(
        np.asarray(mesh.devices).reshape(groups, wide // 2, 2, expert),
        ("groups", "wy", "wc", "expert"),
    )
    rows = ("groups", "wy", "wc")
    in_specs = (
        P(rows, None, "expert"),
        P("groups"),
        P("groups", None),
        P("groups"),
        P("groups"),
        P(),
        P(None, None, GROUP),
        P(None, None, GROUP),
        P(None, WIDE, "expert"),
        P(rows, None, "expert", None),
        P("groups", None, None, GROUP),
    )
    out_specs = P(rows, "expert")
    return jax.shard_map(
        per_device, mesh=split, in_specs=in_specs, out_specs=out_specs, check_vma=False
    )
```

```python
import jax
import jax.numpy as jnp
import numpy as np
from jax import lax
from jax.sharding import Mesh
from jax.sharding import PartitionSpec as P

ADAPTER_SCALE = 0.5

WIDE = ("wy", "wc")
GROUP = ("wy", "wc", "expert")


def per_device(
    prompts,
    span_slot_owner,
    row_expert_index,
    tile_tenant_index,
    tenant_adapter_slot,
    router,
    gate_weight,
    up_weight,
    down_weight,
    adapter_down_weight,
    adapter_up_weight,
):
    span = prompts.shape[1]
    quarter = prompts.shape[2]
    tokens = row_expert_index.shape[0]
    nchunk = tokens // span
    window = gate_weight.shape[0]
    core = lax.axis_index("wc")
    cores = lax.axis_size("wc")
    wide_index = lax.axis_index(WIDE)

    tile_count = tile_tenant_index.shape[0]
    tile_rows = tokens // tile_count
    resident_slots = adapter_down_weight.shape[0]
    rank = adapter_down_weight.shape[3]
    slot_of_span = span_slot_owner[:nchunk]
    held_slots = prompts.shape[0]
    if lax.axis_size("wy") == 2 and cores == 2:
        pair = [(0, 1), (1, 0)]
        slot_chip = lax.ppermute(prompts, "wy", pair)
        slot_core = lax.ppermute(prompts, "wc", pair)
        slot_both = lax.ppermute(slot_chip, "wc", pair)
        slots_q = jnp.concatenate([prompts, slot_core, slot_chip, slot_both], axis=0)
        slot_pick = (
            jnp.bitwise_xor(slot_of_span // held_slots, wide_index) * held_slots
            + slot_of_span % held_slots
        )
    else:
        slots_q = lax.all_gather(prompts, WIDE, axis=0, tiled=True)
        slot_pick = slot_of_span
    rows_q = jnp.take(slots_q, slot_pick, axis=0).reshape(tokens, quarter)

    chips = lax.axis_size("wy")
    tile_slot_index = jnp.take(tenant_adapter_slot, tile_tenant_index)
    holder = tile_slot_index // resident_slots
    local_slot = tile_slot_index % resident_slots
    if chips == 2 and cores == 2:
        swap = [(0, 1), (1, 0)]
        from_chip = lax.ppermute(adapter_down_weight, "wy", swap)
        from_core = lax.ppermute(adapter_down_weight, "wc", swap)
        from_both = lax.ppermute(from_chip, "wc", swap)
        stacked = jnp.stack([adapter_down_weight, from_core, from_chip, from_both])
        source = jnp.bitwise_xor(holder, wide_index)
    else:
        stacked = lax.all_gather(adapter_down_weight, WIDE, axis=0, tiled=False)
        source = holder
    flat_held = stacked.reshape((-1,) + adapter_down_weight.shape[1:])
    tile_adapters = jnp.take(flat_held, source * resident_slots + local_slot, axis=0)

    partial_rank = jnp.einsum(
        "ntd,nedr->nter",
        rows_q.reshape(tile_count, tile_rows, quarter),
        tile_adapters,
        preferred_element_type=jnp.float32,
    ).reshape(tokens, window * rank)
    rank_top = lax.reduce_precision(partial_rank, exponent_bits=8, mantissa_bits=7)
    rank_hi = rank_top.astype(jnp.bfloat16)
    rank_lo = (partial_rank - rank_top).astype(jnp.bfloat16)

    half = tokens // cores
    expert_size = lax.axis_size("expert")
    swap = [(i, (i + 1) % cores) for i in range(cores)]
    mine_q = lax.dynamic_slice_in_dim(rows_q, core * half, half, 0)
    mine = lax.all_gather(mine_q, "expert", axis=1, tiled=True)
    rank_q = lax.dynamic_slice_in_dim(
        jnp.concatenate([rank_hi, rank_lo], axis=1), core * half, half, 0
    )
    rank_q, _ = lax.optimization_barrier((rank_q, mine))
    pieces = lax.all_gather(rank_q, "expert", axis=1, tiled=False).astype(jnp.float32)
    mine_rank = jnp.sum(pieces[:, :, : window * rank] + pieces[:, :, window * rank :], axis=1)
    mine_rank = mine_rank.astype(jnp.bfloat16)
    other = lax.ppermute(mine, "wc", swap)
    other_rank = lax.ppermute(mine_rank, "wc", swap)
    input_rows = jnp.where(
        core == 0, jnp.concatenate([mine, other], axis=0), jnp.concatenate([other, mine], axis=0)
    )
    input_rows = lax.optimization_barrier(input_rows)
    lowrank = jnp.where(
        core == 0,
        jnp.concatenate([mine_rank, other_rank], axis=0),
        jnp.concatenate([other_rank, mine_rank], axis=0),
    ).reshape(tile_count, tile_rows, window, rank)

    logits = jnp.dot(input_rows, router, preferred_element_type=jnp.float32)
    experts = jnp.arange(router.shape[1], dtype=jnp.int32)
    picked = (row_expert_index[:, :, None] == experts[None, None, :]).astype(jnp.float32)
    chosen = jnp.sum(picked * logits[:, None, :], axis=2)
    first_prob = jax.nn.sigmoid(chosen[:, 0] - chosen[:, 1])
    second_prob = jax.nn.sigmoid(chosen[:, 1] - chosen[:, 0])
    weight = (
        first_prob[:, None] * picked[:, 0, :window] + second_prob[:, None] * picked[:, 1, :window]
    )

    tile_up = jnp.take(adapter_up_weight, tile_tenant_index, axis=0)
    adapted_hidden = jnp.einsum(
        "nter,nerf->ntef", lowrank, tile_up, preferred_element_type=jnp.float32
    ).reshape(tokens, window, tile_up.shape[3])

    running = None
    for expert_number in range(window):
        gate_pre = jnp.dot(
            input_rows, gate_weight[expert_number], preferred_element_type=jnp.float32
        )
        up_value = (
            jnp.dot(input_rows, up_weight[expert_number], preferred_element_type=jnp.float32)
            + ADAPTER_SCALE * adapted_hidden[:, expert_number]
        )
        hidden = (
            weight[:, expert_number, None] * jax.nn.silu(gate_pre) * up_value
        ).astype(jnp.bfloat16)
        gathered = lax.all_gather(hidden, "expert", axis=1, tiled=True)
        part = jnp.dot(gathered, down_weight[expert_number], preferred_element_type=jnp.float32)
        running = part if running is None else running + part
    return reduce_rows(running, core, cores).astype(jnp.bfloat16)


def reduce_rows(running, core, cores):
    chips = lax.axis_size("wy")
    block = running.shape[0] // (chips * cores)
    by_chip = running.reshape(chips, cores, block, running.shape[1])
    keep = jnp.where(core == 0, by_chip[:, 0], by_chip[:, 1])
    send = jnp.where(core == 0, by_chip[:, 1], by_chip[:, 0])
    chip_sum = keep + lax.ppermute(send, "wc", [(i, (i + 1) % cores) for i in range(cores)])
    if chips == 2:
        chip = lax.axis_index("wy")
        mine = jnp.where(chip == 0, chip_sum[0], chip_sum[1])
        away = jnp.where(chip == 0, chip_sum[1], chip_sum[0])
        arrived = lax.ppermute(away.astype(jnp.bfloat16), "wy", [(0, 1), (1, 0)])
        return mine + arrived.astype(jnp.float32)
    return lax.psum_scatter(chip_sum, "wy", scatter_dimension=0, tiled=True).reshape(block, -1)


def solution(mesh):
    groups = mesh.shape["groups"]
    wide = mesh.shape["wide"]
    expert = mesh.shape["expert"]
    split = Mesh(
        np.asarray(mesh.devices).reshape(groups, wide // 2, 2, expert),
        ("groups", "wy", "wc", "expert"),
    )
    rows = ("groups", "wy", "wc")
    in_specs = (
        P(rows, None, "expert"),
        P("groups"),
        P("groups", None),
        P("groups"),
        P("groups"),
        P(),
        P(None, None, GROUP),
        P(None, None, GROUP),
        P(None, WIDE, "expert"),
        P(rows, None, "expert", None),
        P("groups", None, None, GROUP),
    )
    out_specs = P(rows, "expert")
    return jax.shard_map(
        per_device, mesh=split, in_specs=in_specs, out_specs=out_specs, check_vma=False
    )
```

```python
import jax
import jax.numpy as jnp
import numpy as np
from jax import lax
from jax.sharding import Mesh
from jax.sharding import PartitionSpec as P

ADAPTER_SCALE = 0.5

WIDE = ("wy", "wc")
GROUP = ("wy", "wc", "expert")


def per_device(
    prompts,
    span_slot_owner,
    row_expert_index,
    tile_tenant_index,
    tenant_adapter_slot,
    router,
    gate_weight,
    up_weight,
    down_weight,
    adapter_down_weight,
    adapter_up_weight,
):
    span = prompts.shape[1]
    quarter = prompts.shape[2]
    tokens = row_expert_index.shape[0]
    nchunk = tokens // span
    window = gate_weight.shape[0]
    core = lax.axis_index("wc")
    cores = lax.axis_size("wc")
    wide_index = lax.axis_index(WIDE)

    tile_count = tile_tenant_index.shape[0]
    tile_rows = tokens // tile_count
    resident_slots = adapter_down_weight.shape[0]
    rank = adapter_down_weight.shape[3]
    slot_of_span = span_slot_owner[:nchunk]
    held_slots = prompts.shape[0]
    if lax.axis_size("wy") == 2 and cores == 2:
        pair = [(0, 1), (1, 0)]
        slot_chip = lax.ppermute(prompts, "wy", pair)
        slot_core = lax.ppermute(prompts, "wc", pair)
        slot_both = lax.ppermute(slot_chip, "wc", pair)
        slots_q = jnp.concatenate([prompts, slot_core, slot_chip, slot_both], axis=0)
        slot_pick = (
            jnp.bitwise_xor(slot_of_span // held_slots, wide_index) * held_slots
            + slot_of_span % held_slots
        )
    else:
        slots_q = lax.all_gather(prompts, WIDE, axis=0, tiled=True)
        slot_pick = slot_of_span
    rows_q = jnp.take(slots_q, slot_pick, axis=0).reshape(tokens, quarter)

    chips = lax.axis_size("wy")
    tile_slot_index = jnp.take(tenant_adapter_slot, tile_tenant_index)
    holder = tile_slot_index // resident_slots
    local_slot = tile_slot_index % resident_slots
    if chips == 2 and cores == 2:
        swap = [(0, 1), (1, 0)]
        from_chip = lax.ppermute(adapter_down_weight, "wy", swap)
        from_core = lax.ppermute(adapter_down_weight, "wc", swap)
        from_both = lax.ppermute(from_chip, "wc", swap)
        stacked = jnp.stack([adapter_down_weight, from_core, from_chip, from_both])
        source = jnp.bitwise_xor(holder, wide_index)
    else:
        stacked = lax.all_gather(adapter_down_weight, WIDE, axis=0, tiled=False)
        source = holder
    flat_held = stacked.reshape((-1,) + adapter_down_weight.shape[1:])
    tile_adapters = jnp.take(flat_held, source * resident_slots + local_slot, axis=0)

    partial_rank = jnp.einsum(
        "ntd,nedr->nter",
        rows_q.reshape(tile_count, tile_rows, quarter),
        tile_adapters,
        preferred_element_type=jnp.float32,
    ).reshape(tokens, window * rank)
    rank_top = lax.reduce_precision(partial_rank, exponent_bits=8, mantissa_bits=7)
    rank_hi = rank_top.astype(jnp.bfloat16)
    rank_lo = (partial_rank - rank_top).astype(jnp.bfloat16)

    half = tokens // cores
    expert_size = lax.axis_size("expert")
    swap = [(i, (i + 1) % cores) for i in range(cores)]
    mine_q = lax.dynamic_slice_in_dim(rows_q, core * half, half, 0)
    mine = lax.all_gather(mine_q, "expert", axis=1, tiled=True)
    rank_q = lax.dynamic_slice_in_dim(
        jnp.concatenate([rank_hi, rank_lo], axis=1), core * half, half, 0
    )
    rank_q, _ = lax.optimization_barrier((rank_q, mine))
    pieces = lax.all_gather(rank_q, "expert", axis=1, tiled=False).astype(jnp.float32)
    mine_rank = jnp.sum(pieces[:, :, : window * rank] + pieces[:, :, window * rank :], axis=1)
    mine_rank = mine_rank.astype(jnp.bfloat16)
    other = lax.ppermute(mine, "wc", swap)
    other_rank = lax.ppermute(mine_rank, "wc", swap)
    input_rows = jnp.where(
        core == 0, jnp.concatenate([mine, other], axis=0), jnp.concatenate([other, mine], axis=0)
    )
    input_rows = lax.optimization_barrier(input_rows)
    lowrank = jnp.where(
        core == 0,
        jnp.concatenate([mine_rank, other_rank], axis=0),
        jnp.concatenate([other_rank, mine_rank], axis=0),
    ).reshape(tile_count, tile_rows, window, rank)

    logits = jnp.dot(input_rows, router, preferred_element_type=jnp.float32)
    experts = jnp.arange(router.shape[1], dtype=jnp.int32)
    picked = (row_expert_index[:, :, None] == experts[None, None, :]).astype(jnp.float32)
    chosen = jnp.sum(picked * logits[:, None, :], axis=2)
    first_prob = jax.nn.sigmoid(chosen[:, 0] - chosen[:, 1])
    second_prob = jax.nn.sigmoid(chosen[:, 1] - chosen[:, 0])
    weight = (
        first_prob[:, None] * picked[:, 0, :window] + second_prob[:, None] * picked[:, 1, :window]
    )

    tile_up = jnp.take(adapter_up_weight, tile_tenant_index, axis=0)
    adapted_hidden = jnp.einsum(
        "nter,nerf->ntef", lowrank, tile_up, preferred_element_type=jnp.float32
    ).reshape(tokens, window, tile_up.shape[3])

    running = None
    for expert_number in range(window):
        gate_pre = jnp.dot(
            input_rows, gate_weight[expert_number], preferred_element_type=jnp.float32
        )
        up_value = (
            jnp.dot(input_rows, up_weight[expert_number], preferred_element_type=jnp.float32)
            + ADAPTER_SCALE * adapted_hidden[:, expert_number]
        )
        hidden = (
            weight[:, expert_number, None] * jax.nn.silu(gate_pre) * up_value
        ).astype(jnp.bfloat16)
        gathered = lax.all_gather(hidden, "expert", axis=1, tiled=True)
        if expert_number == window - 1 and lax.axis_size("wy") == 2 and cores == 2:
            return split_last(gathered, down_weight[expert_number], running, core)
        part = jnp.dot(gathered, down_weight[expert_number], preferred_element_type=jnp.float32)
        running = part if running is None else running + part
    return reduce_rows(running, core, cores).astype(jnp.bfloat16)


def split_last(gathered, down, running, core):
    chip = lax.axis_index("wy")
    span_rows = gathered.shape[0] // 2
    block = span_rows // 2
    pair = [(0, 1), (1, 0)]

    def chip_rows(which, source=gathered):
        part = jnp.dot(
            lax.dynamic_slice_in_dim(source, which * span_rows, span_rows, 0),
            down,
            preferred_element_type=jnp.float32,
        )
        if running is not None:
            part = lax.dynamic_slice_in_dim(running, which * span_rows, span_rows, 0) + part
        keep = lax.dynamic_slice_in_dim(part, core * block, block, 0)
        send = lax.dynamic_slice_in_dim(part, (1 - core) * block, block, 0)
        return keep + lax.ppermute(send, "wc", pair)

    away_sum = chip_rows(1 - chip)
    away = lax.ppermute(away_sum, "wy", pair)
    gathered, _ = lax.optimization_barrier((gathered, away_sum))
    return (chip_rows(chip, gathered) + away).astype(jnp.bfloat16)


def reduce_rows(running, core, cores):
    chips = lax.axis_size("wy")
    block = running.shape[0] // (chips * cores)
    by_chip = running.reshape(chips, cores, block, running.shape[1])
    keep = jnp.where(core == 0, by_chip[:, 0], by_chip[:, 1])
    send = jnp.where(core == 0, by_chip[:, 1], by_chip[:, 0])
    chip_sum = keep + lax.ppermute(send, "wc", [(i, (i + 1) % cores) for i in range(cores)])
    if chips == 2:
        chip = lax.axis_index("wy")
        mine = jnp.where(chip == 0, chip_sum[0], chip_sum[1])
        away = jnp.where(chip == 0, chip_sum[1], chip_sum[0])
        return mine + lax.ppermute(away, "wy", [(0, 1), (1, 0)])
    return lax.psum_scatter(chip_sum, "wy", scatter_dimension=0, tiled=True).reshape(block, -1)


def solution(mesh):
    groups = mesh.shape["groups"]
    wide = mesh.shape["wide"]
    expert = mesh.shape["expert"]
    split = Mesh(
        np.asarray(mesh.devices).reshape(groups, wide // 2, 2, expert),
        ("groups", "wy", "wc", "expert"),
    )
    rows = ("groups", "wy", "wc")
    in_specs = (
        P(rows, None, "expert"),
        P("groups"),
        P("groups", None),
        P("groups"),
        P("groups"),
        P(),
        P(None, None, GROUP),
        P(None, None, GROUP),
        P(None, WIDE, "expert"),
        P(rows, None, "expert", None),
        P("groups", None, None, GROUP),
    )
    out_specs = P(rows, "expert")
    return jax.shard_map(
        per_device, mesh=split, in_specs=in_specs, out_specs=out_specs, check_vma=False
    )
```

```python
import jax
import jax.numpy as jnp
import numpy as np
from jax import lax
from jax.sharding import Mesh
from jax.sharding import PartitionSpec as P

ADAPTER_SCALE = 0.5

WIDE = ("wy", "wc")
GROUP = ("wy", "wc", "expert")


def per_device(
    prompts,
    span_slot_owner,
    row_expert_index,
    tile_tenant_index,
    tenant_adapter_slot,
    router,
    gate_weight,
    up_weight,
    down_weight,
    adapter_down_weight,
    adapter_up_weight,
):
    span = prompts.shape[1]
    quarter = prompts.shape[2]
    tokens = row_expert_index.shape[0]
    nchunk = tokens // span
    window = gate_weight.shape[0]
    core = lax.axis_index("wc")
    cores = lax.axis_size("wc")
    wide_index = lax.axis_index(WIDE)

    tile_count = tile_tenant_index.shape[0]
    tile_rows = tokens // tile_count
    resident_slots = adapter_down_weight.shape[0]
    rank = adapter_down_weight.shape[3]
    slot_of_span = span_slot_owner[:nchunk]
    held_slots = prompts.shape[0]
    if lax.axis_size("wy") == 2 and cores == 2:
        pair = [(0, 1), (1, 0)]
        slot_chip = lax.ppermute(prompts, "wy", pair)
        slot_core = lax.ppermute(prompts, "wc", pair)
        slot_both = lax.ppermute(slot_chip, "wc", pair)
        slots_q = jnp.concatenate([prompts, slot_core, slot_chip, slot_both], axis=0)
        slot_pick = (
            jnp.bitwise_xor(slot_of_span // held_slots, wide_index) * held_slots
            + slot_of_span % held_slots
        )
    else:
        slots_q = lax.all_gather(prompts, WIDE, axis=0, tiled=True)
        slot_pick = slot_of_span
    rows_q = jnp.take(slots_q, slot_pick, axis=0).reshape(tokens, quarter)

    chips = lax.axis_size("wy")
    tile_slot_index = jnp.take(tenant_adapter_slot, tile_tenant_index)
    holder = tile_slot_index // resident_slots
    local_slot = tile_slot_index % resident_slots
    if chips == 2 and cores == 2:
        swap = [(0, 1), (1, 0)]
        from_chip = lax.ppermute(adapter_down_weight, "wy", swap)
        from_core = lax.ppermute(adapter_down_weight, "wc", swap)
        from_both = lax.ppermute(from_chip, "wc", swap)
        stacked = jnp.stack([adapter_down_weight, from_core, from_chip, from_both])
        source = jnp.bitwise_xor(holder, wide_index)
    else:
        stacked = lax.all_gather(adapter_down_weight, WIDE, axis=0, tiled=False)
        source = holder
    flat_held = stacked.reshape((-1,) + adapter_down_weight.shape[1:])
    tile_adapters = jnp.take(flat_held, source * resident_slots + local_slot, axis=0)

    partial_rank = jnp.einsum(
        "ntd,nedr->nter",
        rows_q.reshape(tile_count, tile_rows, quarter),
        tile_adapters,
        preferred_element_type=jnp.float32,
    ).reshape(tokens, window * rank)
    rank_top = lax.reduce_precision(partial_rank, exponent_bits=8, mantissa_bits=7)
    rank_hi = rank_top.astype(jnp.bfloat16)
    rank_lo = (partial_rank - rank_top).astype(jnp.bfloat16)

    half = tokens // cores
    expert_size = lax.axis_size("expert")
    swap = [(i, (i + 1) % cores) for i in range(cores)]
    mine_q = lax.dynamic_slice_in_dim(rows_q, core * half, half, 0)
    mine = lax.all_gather(mine_q, "expert", axis=1, tiled=True)
    rank_q = lax.dynamic_slice_in_dim(
        jnp.concatenate([rank_hi, rank_lo], axis=1), core * half, half, 0
    )
    arrivals = [rank_q] + [
        lax.ppermute(rank_q, "expert", [(i, (i + shift) % expert_size) for i in range(expert_size)])
        for shift in range(1, expert_size)
    ]
    other = lax.ppermute(mine, "wc", swap)
    input_rows = jnp.where(
        core == 0, jnp.concatenate([mine, other], axis=0), jnp.concatenate([other, mine], axis=0)
    )
    input_rows = lax.optimization_barrier(input_rows)
    gate_first = jnp.dot(input_rows, gate_weight[0], preferred_element_type=jnp.float32)
    arrivals, gate_first = lax.optimization_barrier((arrivals, gate_first))
    mine_rank = None
    for piece in arrivals:
        piece = piece.astype(jnp.float32)
        piece = piece[:, : window * rank] + piece[:, window * rank :]
        mine_rank = piece if mine_rank is None else mine_rank + piece
    mine_rank = mine_rank.astype(jnp.bfloat16)
    other_rank = lax.ppermute(mine_rank, "wc", swap)
    lowrank = jnp.where(
        core == 0,
        jnp.concatenate([mine_rank, other_rank], axis=0),
        jnp.concatenate([other_rank, mine_rank], axis=0),
    ).reshape(tile_count, tile_rows, window, rank)

    logits = jnp.dot(input_rows, router, preferred_element_type=jnp.float32)
    experts = jnp.arange(router.shape[1], dtype=jnp.int32)
    picked = (row_expert_index[:, :, None] == experts[None, None, :]).astype(jnp.float32)
    chosen = jnp.sum(picked * logits[:, None, :], axis=2)
    first_prob = jax.nn.sigmoid(chosen[:, 0] - chosen[:, 1])
    second_prob = jax.nn.sigmoid(chosen[:, 1] - chosen[:, 0])
    weight = (
        first_prob[:, None] * picked[:, 0, :window] + second_prob[:, None] * picked[:, 1, :window]
    )

    tile_up = jnp.take(adapter_up_weight, tile_tenant_index, axis=0)
    adapted_hidden = jnp.einsum(
        "nter,nerf->ntef", lowrank, tile_up, preferred_element_type=jnp.float32
    ).reshape(tokens, window, tile_up.shape[3])

    running = None
    for expert_number in range(window):
        gate_pre = gate_first if expert_number == 0 else jnp.dot(
            input_rows, gate_weight[expert_number], preferred_element_type=jnp.float32
        )
        up_value = (
            jnp.dot(input_rows, up_weight[expert_number], preferred_element_type=jnp.float32)
            + ADAPTER_SCALE * adapted_hidden[:, expert_number]
        )
        hidden = (
            weight[:, expert_number, None] * jax.nn.silu(gate_pre) * up_value
        ).astype(jnp.bfloat16)
        gathered = lax.all_gather(hidden, "expert", axis=1, tiled=True)
        if expert_number == window - 1 and lax.axis_size("wy") == 2 and cores == 2:
            return split_last(gathered, down_weight[expert_number], running, core)
        part = jnp.dot(gathered, down_weight[expert_number], preferred_element_type=jnp.float32)
        running = part if running is None else running + part
    return reduce_rows(running, core, cores).astype(jnp.bfloat16)


def split_last(gathered, down, running, core):
    chip = lax.axis_index("wy")
    span_rows = gathered.shape[0] // 2
    block = span_rows // 2
    pair = [(0, 1), (1, 0)]

    def chip_rows(which, source=gathered):
        part = jnp.dot(
            lax.dynamic_slice_in_dim(source, which * span_rows, span_rows, 0),
            down,
            preferred_element_type=jnp.float32,
        )
        if running is not None:
            part = lax.dynamic_slice_in_dim(running, which * span_rows, span_rows, 0) + part
        keep = lax.dynamic_slice_in_dim(part, core * block, block, 0)
        send = lax.dynamic_slice_in_dim(part, (1 - core) * block, block, 0)
        return keep + lax.ppermute(send, "wc", pair)

    away_sum = chip_rows(1 - chip)
    away = lax.ppermute(away_sum, "wy", pair)
    gathered, _ = lax.optimization_barrier((gathered, away_sum))
    return (chip_rows(chip, gathered) + away).astype(jnp.bfloat16)


def reduce_rows(running, core, cores):
    chips = lax.axis_size("wy")
    block = running.shape[0] // (chips * cores)
    by_chip = running.reshape(chips, cores, block, running.shape[1])
    keep = jnp.where(core == 0, by_chip[:, 0], by_chip[:, 1])
    send = jnp.where(core == 0, by_chip[:, 1], by_chip[:, 0])
    chip_sum = keep + lax.ppermute(send, "wc", [(i, (i + 1) % cores) for i in range(cores)])
    if chips == 2:
        chip = lax.axis_index("wy")
        mine = jnp.where(chip == 0, chip_sum[0], chip_sum[1])
        away = jnp.where(chip == 0, chip_sum[1], chip_sum[0])
        return mine + lax.ppermute(away, "wy", [(0, 1), (1, 0)])
    return lax.psum_scatter(chip_sum, "wy", scatter_dimension=0, tiled=True).reshape(block, -1)


def solution(mesh):
    groups = mesh.shape["groups"]
    wide = mesh.shape["wide"]
    expert = mesh.shape["expert"]
    split = Mesh(
        np.asarray(mesh.devices).reshape(groups, wide // 2, 2, expert),
        ("groups", "wy", "wc", "expert"),
    )
    rows = ("groups", "wy", "wc")
    in_specs = (
        P(rows, None, "expert"),
        P("groups"),
        P("groups", None),
        P("groups"),
        P("groups"),
        P(),
        P(None, None, GROUP),
        P(None, None, GROUP),
        P(None, WIDE, "expert"),
        P(rows, None, "expert", None),
        P("groups", None, None, GROUP),
    )
    out_specs = P(rows, "expert")
    return jax.shard_map(
        per_device, mesh=split, in_specs=in_specs, out_specs=out_specs, check_vma=False
    )
```

```python
import jax
import jax.numpy as jnp
import numpy as np
from jax import lax
from jax.sharding import Mesh
from jax.sharding import PartitionSpec as P

ADAPTER_SCALE = 0.5

WIDE = ("wy", "wc")
GROUP = ("wy", "wc", "expert")


def per_device(
    prompts,
    span_slot_owner,
    row_expert_index,
    tile_tenant_index,
    tenant_adapter_slot,
    router,
    gate_weight,
    up_weight,
    down_weight,
    adapter_down_weight,
    adapter_up_weight,
):
    span = prompts.shape[1]
    quarter = prompts.shape[2]
    tokens = row_expert_index.shape[0]
    nchunk = tokens // span
    window = gate_weight.shape[0]
    core = lax.axis_index("wc")
    cores = lax.axis_size("wc")
    wide_index = lax.axis_index(WIDE)

    tile_count = tile_tenant_index.shape[0]
    tile_rows = tokens // tile_count
    resident_slots = adapter_down_weight.shape[0]
    rank = adapter_down_weight.shape[3]
    slot_of_span = span_slot_owner[:nchunk]
    held_slots = prompts.shape[0]
    if lax.axis_size("wy") == 2 and cores == 2:
        pair = [(0, 1), (1, 0)]
        slot_chip = lax.ppermute(prompts, "wy", pair)
        slot_core = lax.ppermute(prompts, "wc", pair)
        slot_both = lax.ppermute(slot_chip, "wc", pair)
        slots_q = jnp.concatenate([prompts, slot_core, slot_chip, slot_both], axis=0)
        slot_pick = (
            jnp.bitwise_xor(slot_of_span // held_slots, wide_index) * held_slots
            + slot_of_span % held_slots
        )
    else:
        slots_q = lax.all_gather(prompts, WIDE, axis=0, tiled=True)
        slot_pick = slot_of_span
    rows_q = jnp.take(slots_q, slot_pick, axis=0).reshape(tokens, quarter)

    chips = lax.axis_size("wy")
    tile_slot_index = jnp.take(tenant_adapter_slot, tile_tenant_index)
    holder = tile_slot_index // resident_slots
    local_slot = tile_slot_index % resident_slots
    if chips == 2 and cores == 2:
        swap = [(0, 1), (1, 0)]
        from_chip = lax.ppermute(adapter_down_weight, "wy", swap)
        from_core = lax.ppermute(adapter_down_weight, "wc", swap)
        from_both = lax.ppermute(from_chip, "wc", swap)
        stacked = jnp.stack([adapter_down_weight, from_core, from_chip, from_both])
        source = jnp.bitwise_xor(holder, wide_index)
    else:
        stacked = lax.all_gather(adapter_down_weight, WIDE, axis=0, tiled=False)
        source = holder
    flat_held = stacked.reshape((-1,) + adapter_down_weight.shape[1:])
    tile_adapters = jnp.take(flat_held, source * resident_slots + local_slot, axis=0)

    partial_rank = jnp.einsum(
        "ntd,nedr->nter",
        rows_q.reshape(tile_count, tile_rows, quarter),
        tile_adapters,
        preferred_element_type=jnp.float32,
    ).reshape(tokens, window * rank)
    rank_top = lax.reduce_precision(partial_rank, exponent_bits=8, mantissa_bits=7)
    rank_hi = rank_top.astype(jnp.bfloat16)
    rank_lo = (partial_rank - rank_top).astype(jnp.bfloat16)

    half = tokens // cores
    expert_size = lax.axis_size("expert")
    swap = [(i, (i + 1) % cores) for i in range(cores)]
    mine_q = lax.dynamic_slice_in_dim(rows_q, core * half, half, 0)
    mine = lax.all_gather(mine_q, "expert", axis=1, tiled=True)
    rank_q = lax.dynamic_slice_in_dim(
        jnp.concatenate([rank_hi, rank_lo], axis=1), core * half, half, 0
    )
    rank_q, _ = lax.optimization_barrier((rank_q, mine))
    pieces = lax.all_gather(rank_q, "expert", axis=1, tiled=False).astype(jnp.float32)
    mine_rank = jnp.sum(pieces[:, :, : window * rank] + pieces[:, :, window * rank :], axis=1)
    mine_rank = mine_rank.astype(jnp.bfloat16)
    other = lax.ppermute(mine, "wc", swap)
    other_rank = lax.ppermute(mine_rank, "wc", swap)
    input_rows = lax.dynamic_slice_in_dim(
        jnp.concatenate([mine, other, mine], axis=0), core * half, tokens, 0
    )
    input_rows = lax.optimization_barrier(input_rows)
    lowrank = jnp.where(
        core == 0,
        jnp.concatenate([mine_rank, other_rank], axis=0),
        jnp.concatenate([other_rank, mine_rank], axis=0),
    ).reshape(tile_count, tile_rows, window, rank)

    logits = jnp.dot(input_rows, router, preferred_element_type=jnp.float32)
    experts = jnp.arange(router.shape[1], dtype=jnp.int32)
    picked = (row_expert_index[:, :, None] == experts[None, None, :]).astype(jnp.float32)
    chosen = jnp.sum(picked * logits[:, None, :], axis=2)
    first_prob = jax.nn.sigmoid(chosen[:, 0] - chosen[:, 1])
    second_prob = jax.nn.sigmoid(chosen[:, 1] - chosen[:, 0])
    weight = (
        first_prob[:, None] * picked[:, 0, :window] + second_prob[:, None] * picked[:, 1, :window]
    )

    tile_up = jnp.take(adapter_up_weight, tile_tenant_index, axis=0)
    adapted_hidden = jnp.einsum(
        "nter,nerf->ntef", lowrank, tile_up, preferred_element_type=jnp.float32
    ).reshape(tokens, window, tile_up.shape[3])

    running = None
    for expert_number in range(window):
        gate_pre = jnp.dot(
            input_rows, gate_weight[expert_number], preferred_element_type=jnp.float32
        )
        up_value = (
            jnp.dot(input_rows, up_weight[expert_number], preferred_element_type=jnp.float32)
            + ADAPTER_SCALE * adapted_hidden[:, expert_number]
        )
        hidden = (
            weight[:, expert_number, None] * jax.nn.silu(gate_pre) * up_value
        ).astype(jnp.bfloat16)
        gathered = lax.all_gather(hidden, "expert", axis=1, tiled=True)
        if expert_number == window - 1 and lax.axis_size("wy") == 2 and cores == 2:
            return split_last(gathered, down_weight[expert_number], running, core)
        part = jnp.dot(gathered, down_weight[expert_number], preferred_element_type=jnp.float32)
        running = part if running is None else running + part
    return reduce_rows(running, core, cores).astype(jnp.bfloat16)


def split_last(gathered, down, running, core):
    chip = lax.axis_index("wy")
    span_rows = gathered.shape[0] // 2
    block = span_rows // 2
    pair = [(0, 1), (1, 0)]

    def chip_rows(which, source=gathered):
        part = jnp.dot(
            lax.dynamic_slice_in_dim(source, which * span_rows, span_rows, 0),
            down,
            preferred_element_type=jnp.float32,
        )
        if running is not None:
            part = lax.dynamic_slice_in_dim(running, which * span_rows, span_rows, 0) + part
        keep = lax.dynamic_slice_in_dim(part, core * block, block, 0)
        send = lax.dynamic_slice_in_dim(part, (1 - core) * block, block, 0)
        return keep + lax.ppermute(send, "wc", pair)

    away_sum = chip_rows(1 - chip)
    away = lax.ppermute(away_sum, "wy", pair)
    gathered, _ = lax.optimization_barrier((gathered, away_sum))
    return (chip_rows(chip, gathered) + away).astype(jnp.bfloat16)


def reduce_rows(running, core, cores):
    chips = lax.axis_size("wy")
    block = running.shape[0] // (chips * cores)
    by_chip = running.reshape(chips, cores, block, running.shape[1])
    keep = jnp.where(core == 0, by_chip[:, 0], by_chip[:, 1])
    send = jnp.where(core == 0, by_chip[:, 1], by_chip[:, 0])
    chip_sum = keep + lax.ppermute(send, "wc", [(i, (i + 1) % cores) for i in range(cores)])
    if chips == 2:
        chip = lax.axis_index("wy")
        mine = jnp.where(chip == 0, chip_sum[0], chip_sum[1])
        away = jnp.where(chip == 0, chip_sum[1], chip_sum[0])
        return mine + lax.ppermute(away, "wy", [(0, 1), (1, 0)])
    return lax.psum_scatter(chip_sum, "wy", scatter_dimension=0, tiled=True).reshape(block, -1)


def solution(mesh):
    groups = mesh.shape["groups"]
    wide = mesh.shape["wide"]
    expert = mesh.shape["expert"]
    split = Mesh(
        np.asarray(mesh.devices).reshape(groups, wide // 2, 2, expert),
        ("groups", "wy", "wc", "expert"),
    )
    rows = ("groups", "wy", "wc")
    in_specs = (
        P(rows, None, "expert"),
        P("groups"),
        P("groups", None),
        P("groups"),
        P("groups"),
        P(),
        P(None, None, GROUP),
        P(None, None, GROUP),
        P(None, WIDE, "expert"),
        P(rows, None, "expert", None),
        P("groups", None, None, GROUP),
    )
    out_specs = P(rows, "expert")
    return jax.shard_map(
        per_device, mesh=split, in_specs=in_specs, out_specs=out_specs, check_vma=False
    )
```
